768 devices in a mesh: grp: 96 (over z, x, core), blk: 8 (over y).
Axes of the slice: x: 4, y: 8, z: 12, core: 2. Of those that a mesh axis runs over, the one named last changes fastest.
Arguments:
- query: bfloat16 [196608, 512], P(('grp', 'blk')), may hold values from -6 to 6
- key: bfloat16 [196608, 512], P(('grp', 'blk')), may hold values from -6 to 6
- value: bfloat16 [196608, 512], P(('grp', 'blk')), may hold values from -6 to 6
- out_grad: bfloat16 [196608, 512], P(('grp', 'blk')), may hold values from -6 to 6
- partner: int32 [2, 196608], P(None, ('grp', 'blk')), may hold values from 0 to 127, as said below
- tiles: int32 [1536, 6], P(('grp', 'blk')), may hold values from 0 to 15, as said below
- tile_count: int32 [1536], P(('grp', 'blk')), may hold values from 1 to 6, as said below
Outputs:
- attended: bfloat16 [196608, 512], P(('grp', 'blk'))
- query_grad: bfloat16 [196608, 512], P(('grp', 'blk'))
- key_grad: bfloat16 [196608, 512], P(('grp', 'blk'))
- value_grad: bfloat16 [196608, 512], P(('grp', 'blk'))
The draws below stay inside these ranges and needn't reach their ends.
Inputs may be any that keep to these rules, and one draw needn't show every extreme that they name: `partner`: the matching of every round is symmetric: match[r, match[r, n]] = n for every node n. `tiles`: the entries of a row are distinct; the first entry of block k's row is k's own block within its cluster; block a lists block b among its first tile_count entries exactly when b lists a. `tile_count`: some block of every cluster uses all 6 slots.
All inputs are finite; a program needn't handle non-finite values.
Results may differ from the reference program's by a relative error of at most 0.014.
Values may be sent and summed in bfloat16 or wider, within the bound.
No kernel may reach another device: no remote copies, remote signals or barrier semaphores. Data moves between devices by JAX's collectives and lax.ppermute only.
A program may use at most 64 MiB of HBM per device.

```python
import jax
import jax.numpy as jnp
from jax import lax

D = 512
HEADS = 8
HEAD_DIM = 64
NODE_DEV = 256
BLOCK = 128
TMAX = 6
ROUNDS = 2
CLUSTER = 2048
NODES = 196608


def paired_rows(key):
    base = jax.random.fold_in(key, 7)
    queries = jnp.clip(jax.random.normal(jax.random.fold_in(base, 1), (NODES, D), jnp.float32), -6.0, 6.0)
    keys = jnp.clip(jax.random.normal(jax.random.fold_in(base, 2), (NODES, D), jnp.float32), -6.0, 6.0)
    return (queries, keys)


def draw_query(key, part):
    return paired_rows(key)[0].astype(jnp.bfloat16)


def draw_key(key, part):
    return paired_rows(key)[1].astype(jnp.bfloat16)


def draw_partner(key, part):
    base = jax.random.fold_in(key, 21)
    units = NODES // NODE_DEV
    per_cluster = CLUSTER // NODE_DEV
    clusters = NODES // CLUSTER
    half = NODE_DEV // 2
    unit = jnp.arange(units, dtype=jnp.int32)
    owner = unit // per_cluster
    rank = unit % per_cluster

    def one_perm(subkey):
        return jax.random.permutation(subkey, half).astype(jnp.int32)
    table = []
    for step in range(ROUNDS):
        subkeys = jax.random.split(jax.random.fold_in(base, step), units)
        forward = jax.vmap(one_perm)(subkeys)
        inverse = jnp.argsort(forward, axis=1, stable=True).astype(jnp.int32)
        behind = (owner - step - 1) % clusters * per_cluster + rank
        second = inverse[behind]
        table.append(jnp.concatenate([forward, second], 1).reshape(NODES))
    return jnp.stack(table).astype(jnp.int32)


def block_links(key):
    base = jax.random.fold_in(key, 33)
    blocks = CLUSTER // BLOCK
    clusters = NODES // CLUSTER
    cycle = blocks - 1

    def one_cluster(subkey):
        first_key, second_key, third_key = jax.random.split(subkey, 3)
        rounds = jax.random.permutation(first_key, cycle)[:TMAX - 1].astype(jnp.int32)
        label = jax.random.permutation(second_key, blocks).astype(jnp.int32)
        place = jnp.argsort(label, stable=True).astype(jnp.int32)
        flips = jax.random.randint(third_key, (TMAX - 1, blocks), 0, 2).astype(jnp.int32)
        spot = place[None, :]
        turn = rounds[:, None]
        mate = jnp.where(spot == cycle, turn, jnp.where(spot == turn, cycle, (2 * turn - spot) % cycle))
        lower = jnp.minimum(spot, mate)
        keep = (jnp.take_along_axis(flips, lower, axis=1) == 1) | (spot == 0) | (mate == 0)
        entries = label[mate]
        candidates = jnp.concatenate([jnp.arange(blocks, dtype=jnp.int32)[None, :], entries], 0).T
        flags = jnp.concatenate([jnp.ones((1, blocks), jnp.int32), keep.astype(jnp.int32)], 0).T
        order = jnp.argsort(1 - flags, axis=1, stable=True)
        chosen = jnp.take_along_axis(candidates, order, axis=1)
        return (chosen.astype(jnp.int32), jnp.sum(flags, 1).astype(jnp.int32))
    subkeys = jax.random.split(base, clusters)
    chosen, counted = jax.vmap(one_cluster)(subkeys)
    return (chosen.reshape(clusters * blocks, TMAX).astype(jnp.int32), counted.reshape(clusters * blocks).astype(jnp.int32))


def draw_tiles(key, part):
    return block_links(key)[0]


def draw_tile_count(key, part):
    return block_links(key)[1]


def shard_levels(own_key, extent, cuts, low, high):
    loudness, own = 1.0, jax.random.fold_in(own_key, 6)
    for axis_at, parts in cuts:
        heights = jnp.exp(jax.random.uniform(jax.random.fold_in(own, axis_at), (parts,), jnp.float32, low / len(cuts), high / len(cuts)))
        loudness = loudness * jnp.repeat(heights, extent[axis_at] // parts).reshape([-1 if axis == axis_at else 1 for axis in range(len(extent))])
    return loudness


def scatter_about(key, dims, width, most, shards=(), kind=jnp.bfloat16):
    level = shard_levels(key, dims, shards, -0.22, 0.18) if shards else 1.0
    result = jax.random.normal(key, dims, jnp.float32) * width * level
    return jnp.minimum(jnp.maximum(result, -most), most).astype(kind)


def setup_inputs(seed: int = 0) -> dict:
    streams_of = jax.random.split(jax.random.key(seed), 8)
    query = draw_query(jax.random.fold_in(streams_of[7], 71), 0)
    key = draw_key(jax.random.fold_in(streams_of[7], 71), 0)
    value = scatter_about(streams_of[2], (NODES, D), 1.0, 6.0, ((0, 768),))
    out_grad = scatter_about(streams_of[3], (NODES, D), 1.0, 6.0, ((0, 768),))
    partner = draw_partner(jax.random.fold_in(streams_of[7], 71), 0)
    tiles = draw_tiles(jax.random.fold_in(streams_of[7], 71), 0)
    tile_count = draw_tile_count(jax.random.fold_in(streams_of[7], 71), 0)
    return dict(query=query, key=key, value=value, out_grad=out_grad, partner=partner, tiles=tiles, tile_count=tile_count)


NEG_BIG = -1.0e30


def settle(values):
    return lax.optimization_barrier(values.astype(jnp.bfloat16)).astype(jnp.float32)


def match_table(partner):
    per_cluster = CLUSTER // NODE_DEV
    clusters = NODES // CLUSTER
    half = NODE_DEV // 2
    node = jnp.arange(NODES, dtype=jnp.int32)
    unit = node // NODE_DEV
    owner = unit // per_cluster
    rank = unit % per_cluster
    first_half = (node % NODE_DEV) < half
    table = []
    for step in range(ROUNDS):
        ahead = ((owner + step + 1) % clusters) * per_cluster + rank
        behind = ((owner - step - 1) % clusters) * per_cluster + rank
        target = jnp.where(first_half, ahead * NODE_DEV + half + partner[step], behind * NODE_DEV + partner[step])
        table.append(target.astype(jnp.int32))
    return jnp.stack(table)


def cluster_pass(index, query, key, value, out_grad, match, tiles, tile_count):
    f32 = jnp.float32
    blocks = CLUSTER // BLOCK
    units = CLUSTER // NODE_DEV
    per_unit = NODE_DEV // BLOCK
    keys_tile = TMAX * BLOCK
    scale = HEAD_DIM ** -0.5
    first = index * CLUSTER

    def cluster_rows(array):
        return lax.dynamic_slice_in_dim(array, first, CLUSTER, 0)

    tile_ids = lax.dynamic_slice_in_dim(tiles, index * blocks, blocks, 0)
    tile_num = lax.dynamic_slice_in_dim(tile_count, index * blocks, blocks, 0)
    mates = lax.dynamic_slice_in_dim(match, first, CLUSTER, 1)
    shape = (blocks, BLOCK, HEADS, HEAD_DIM)
    q_f = cluster_rows(query).astype(f32).reshape(shape)
    g_f = cluster_rows(out_grad).astype(f32).reshape(shape)
    k_tile = cluster_rows(key).reshape(blocks, BLOCK, D)[tile_ids].astype(f32).reshape(blocks, keys_tile, HEADS, HEAD_DIM)
    v_tile = cluster_rows(value).reshape(blocks, BLOCK, D)[tile_ids].astype(f32).reshape(blocks, keys_tile, HEADS, HEAD_DIM)
    pair_shape = (ROUNDS, blocks, BLOCK, HEADS, HEAD_DIM)
    k_pair = key[mates].astype(f32).reshape(pair_shape)
    v_pair = value[mates].astype(f32).reshape(pair_shape)
    live = jnp.arange(TMAX, dtype=jnp.int32)[None, :] < tile_num[:, None]
    key_live = jnp.broadcast_to(live[:, :, None], (blocks, TMAX, BLOCK)).reshape(blocks, keys_tile)

    s_loc = jnp.einsum("bqhd,bkhd->bhqk", q_f, k_tile) * scale
    s_loc = jnp.where(key_live[:, None, None, :], s_loc, NEG_BIG)
    s_pair = jnp.einsum("bqhd,rbqhd->bhqr", q_f, k_pair) * scale
    top = jnp.maximum(jnp.max(s_loc, -1), jnp.max(s_pair, -1))
    e_loc = jnp.exp(s_loc - top[..., None])
    e_pair = jnp.exp(s_pair - top[..., None])
    total = jnp.sum(e_loc, -1) + jnp.sum(e_pair, -1)
    p_loc = e_loc / total[..., None]
    p_pair = e_pair / total[..., None]
    w_loc = settle(p_loc)
    w_pair = settle(p_pair)
    out_full = jnp.einsum("bhqk,bkhd->bqhd", w_loc, v_tile) + jnp.einsum("bhqr,rbqhd->bqhd", w_pair, v_pair)
    delta = jnp.transpose(jnp.sum(g_f * out_full, -1), (0, 2, 1))
    d_loc = jnp.einsum("bqhd,bkhd->bhqk", g_f, v_tile)
    d_pair = jnp.einsum("bqhd,rbqhd->bhqr", g_f, v_pair)
    z_loc = settle(p_loc * (d_loc - delta[..., None]))
    z_pair = settle(p_pair * (d_pair - delta[..., None]))
    q_grad = (jnp.einsum("bhqk,bkhd->bqhd", z_loc, k_tile) + jnp.einsum("bhqr,rbqhd->bqhd", z_pair, k_pair)) * scale
    c_key = (jnp.einsum("bhqk,bqhd->bkhd", z_loc, q_f) * scale).reshape(units, per_unit, TMAX, BLOCK, D)
    c_val = jnp.einsum("bhqk,bqhd->bkhd", w_loc, g_f).reshape(units, per_unit, TMAX, BLOCK, D)
    unit_ids = tile_ids.reshape(units, per_unit, TMAX)

    def spread_unit(ids_one, values_one):
        return jnp.zeros((blocks, BLOCK, D), f32).at[ids_one].add(values_one)

    part_key = jnp.sum(settle(jax.vmap(spread_unit)(unit_ids, c_key)), 0).reshape(CLUSTER, D)
    part_val = jnp.sum(settle(jax.vmap(spread_unit)(unit_ids, c_val)), 0).reshape(CLUSTER, D)
    term_key = (jnp.einsum("bhqr,bqhd->rbqhd", z_pair, q_f) * scale).astype(jnp.bfloat16).reshape(ROUNDS, CLUSTER, D)
    term_val = jnp.einsum("bhqr,bqhd->rbqhd", w_pair, g_f).astype(jnp.bfloat16).reshape(ROUNDS, CLUSTER, D)
    attended = out_full.reshape(CLUSTER, D).astype(jnp.bfloat16)
    query_grad = q_grad.reshape(CLUSTER, D).astype(jnp.bfloat16)
    return attended, query_grad, part_key, part_val, term_key, term_val


def reference(query, key, value, out_grad, partner, tiles, tile_count):
    match = match_table(partner)
    clusters = NODES // CLUSTER

    def run_cluster(index):
        return cluster_pass(index, query, key, value, out_grad, match, tiles, tile_count)

    attended, query_grad, part_key, part_val, term_key, term_val = lax.map(run_cluster, jnp.arange(clusters, dtype=jnp.int32))
    attended = attended.reshape(NODES, D)
    query_grad = query_grad.reshape(NODES, D)
    term_key = jnp.moveaxis(term_key, 1, 0).reshape(ROUNDS, NODES, D)
    term_val = jnp.moveaxis(term_val, 1, 0).reshape(ROUNDS, NODES, D)
    back_key = part_key.reshape(NODES, D)
    back_val = part_val.reshape(NODES, D)
    for step in range(ROUNDS):
        back_key = back_key + term_key[step][match[step]].astype(jnp.float32)
        back_val = back_val + term_val[step][match[step]].astype(jnp.float32)
    return attended, query_grad, back_key.astype(jnp.bfloat16), back_val.astype(jnp.bfloat16)
```

```python
import jax
import jax.numpy as jnp
from jax import lax
from jax.sharding import PartitionSpec as P

HEADS = 8
BLOCK = 128
TMAX = 6
ROUNDS = 2


NEG_BIG = -1e30


def passed_along(x, axis, by):
    size = lax.axis_size(axis)
    return lax.ppermute(x, axis, [(i, (i + by) % size) for i in range(size)])


def fetch_partners(load, slots, offset):
    half = load.shape[0] // 2
    ahead = passed_along(load[half:], "grp", -offset)
    behind = passed_along(load[:half], "grp", offset)
    return jnp.concatenate([ahead[slots[:half]], behind[slots[half:]]], 0)


def shards(query, key, value, out_grad, partner, tiles, tile_count):
    f32 = jnp.float32
    bf16 = jnp.bfloat16
    nodes, width = query.shape
    head_dim = width // HEADS
    scale = head_dim ** (-0.5)
    blocks_dev = nodes // BLOCK
    team = lax.axis_size("blk")
    cluster_blocks = blocks_dev * team
    keys_tile = TMAX * BLOCK
    heads4 = (blocks_dev, BLOCK, HEADS, head_dim)

    both = jnp.concatenate([key, value], 1)
    kv_cluster = lax.all_gather(both, "blk", axis=0, tiled=True)
    qg_cluster = lax.all_gather(jnp.concatenate([query, out_grad], 1), "blk", axis=0, tiled=True)
    partner_rows = jnp.stack(
        [fetch_partners(both, partner[step], step + 1) for step in range(ROUNDS)]
    )
    live = jnp.arange(TMAX, dtype=jnp.int32)[None, :] < tile_count[:, None]
    tile_live = jnp.broadcast_to(live[:, :, None], (blocks_dev, TMAX, BLOCK)).reshape(
        blocks_dev, keys_tile
    )

    kv_tiles = kv_cluster.reshape(cluster_blocks, BLOCK, 2 * width)[tiles].reshape(
        blocks_dev, keys_tile, 2 * width
    )
    k_tile = kv_tiles[..., :width].reshape(blocks_dev, keys_tile, HEADS, head_dim)
    v_tile = kv_tiles[..., width:].reshape(blocks_dev, keys_tile, HEADS, head_dim)
    pair_shape = (ROUNDS,) + heads4
    k_pair = partner_rows[..., :width].reshape(pair_shape)
    v_pair = partner_rows[..., width:].reshape(pair_shape)
    q4 = query.reshape(heads4)
    g4 = out_grad.reshape(heads4)

    s_loc = jnp.einsum("bqhd,bkhd->bhqk", q4, k_tile, preferred_element_type=f32) * scale
    s_loc = jnp.where(tile_live[:, None, None, :], s_loc, NEG_BIG)
    s_pair = jnp.einsum("bqhd,rbqhd->bhqr", q4, k_pair, preferred_element_type=f32) * scale
    top = jnp.maximum(jnp.max(s_loc, -1), jnp.max(s_pair, -1))
    e_loc = jnp.exp(s_loc - top[..., None])
    e_pair = jnp.exp(s_pair - top[..., None])
    total = jnp.sum(e_loc, -1) + jnp.sum(e_pair, -1)
    p_loc = e_loc / total[..., None]
    p_pair = e_pair / total[..., None]
    w_loc = p_loc.astype(bf16)
    w_pair = p_pair.astype(bf16)
    out_full = jnp.einsum("bhqk,bkhd->bqhd", w_loc, v_tile, preferred_element_type=f32)
    out_full = out_full + jnp.einsum("bhqr,rbqhd->bqhd", w_pair, v_pair, preferred_element_type=f32)
    delta = jnp.transpose(jnp.sum(g4.astype(f32) * out_full, -1), (0, 2, 1))
    d_loc = jnp.einsum("bqhd,bkhd->bhqk", g4, v_tile, preferred_element_type=f32)
    d_pair = jnp.einsum("bqhd,rbqhd->bhqr", g4, v_pair, preferred_element_type=f32)
    z_loc = (p_loc * (d_loc - delta[..., None])).astype(bf16)
    z_pair = (p_pair * (d_pair - delta[..., None])).astype(bf16)
    q_grad = jnp.einsum("bhqk,bkhd->bqhd", z_loc, k_tile, preferred_element_type=f32)
    q_grad = (
        q_grad + jnp.einsum("bhqr,rbqhd->bqhd", z_pair, k_pair, preferred_element_type=f32)
    ) * scale
    t_key = (
        jnp.einsum("bhqr,bqhd->rbqhd", z_pair, q4, preferred_element_type=f32) * scale
    ).astype(bf16)
    t_val = jnp.einsum("bhqr,bqhd->rbqhd", w_pair, g4, preferred_element_type=f32).astype(bf16)
    terms = jnp.concatenate(
        [t_key.reshape(ROUNDS, nodes, width), t_val.reshape(ROUNDS, nodes, width)], 2
    )
    returned = jnp.stack(
        [fetch_partners(terms[step], partner[step], step + 1) for step in range(ROUNDS)]
    )
    returned = jnp.sum(returned.astype(f32), 0)

    stats = jnp.stack([top, total, delta], 1)
    stats = jnp.transpose(stats, (0, 3, 1, 2)).reshape(nodes, 3 * HEADS)
    stats_cluster = lax.all_gather(stats, "blk", axis=0, tiled=True)

    qg_tiles = qg_cluster.reshape(cluster_blocks, BLOCK, 2 * width)[tiles].reshape(
        blocks_dev, keys_tile, 2 * width
    )
    q_tile = qg_tiles[..., :width].reshape(blocks_dev, keys_tile, HEADS, head_dim)
    g_tile = qg_tiles[..., width:].reshape(blocks_dev, keys_tile, HEADS, head_dim)
    st = stats_cluster.reshape(cluster_blocks, BLOCK, 3, HEADS)[tiles].reshape(
        blocks_dev, keys_tile, 3, HEADS
    )
    st = jnp.transpose(st, (0, 2, 3, 1))
    top_t, total_t, delta_t = st[:, 0], st[:, 1], st[:, 2]
    k4 = key.reshape(heads4)
    v4 = value.reshape(heads4)
    s_key = jnp.einsum("bkhd,bqhd->bhkq", k4, q_tile, preferred_element_type=f32) * scale
    s_key = jnp.where(tile_live[:, None, None, :], s_key, NEG_BIG)
    p_key = jnp.exp(s_key - top_t[:, :, None, :]) / total_t[:, :, None, :]
    w_key = p_key.astype(bf16)
    d_key = jnp.einsum("bkhd,bqhd->bhkq", v4, g_tile, preferred_element_type=f32)
    z_key = (p_key * (d_key - delta_t[:, :, None, :])).astype(bf16)
    k_sum = jnp.einsum("bhkq,bqhd->bkhd", z_key, q_tile, preferred_element_type=f32) * scale
    v_sum = jnp.einsum("bhkq,bqhd->bkhd", w_key, g_tile, preferred_element_type=f32)

    attended = out_full.reshape(nodes, width).astype(bf16)
    query_grad = q_grad.reshape(nodes, width).astype(bf16)
    key_grad = (k_sum.reshape(nodes, width) + returned[:, :width]).astype(bf16)
    value_grad = (v_sum.reshape(nodes, width) + returned[:, width:]).astype(bf16)
    return (attended, query_grad, key_grad, value_grad)


def solution(mesh):
    in_specs = (
        P(("grp", "blk"), None),
        P(("grp", "blk"), None),
        P(("grp", "blk"), None),
        P(("grp", "blk"), None),
        P(None, ("grp", "blk")),
        P(("grp", "blk"), None),
        P(("grp", "blk")),
    )
    out_specs = (
        P(("grp", "blk"), None),
        P(("grp", "blk"), None),
        P(("grp", "blk"), None),
        P(("grp", "blk"), None),
    )
    return jax.shard_map(shards, mesh=mesh, in_specs=in_specs, out_specs=out_specs, check_vma=False)
```

```python
import jax
import jax.numpy as jnp
from jax import lax
from jax.sharding import PartitionSpec as P

HEADS = 8
BLOCK = 128
TMAX = 6
ROUNDS = 2


NEG_BIG = -1e30


def passed_along(x, axis, by):
    size = lax.axis_size(axis)
    return lax.ppermute(x, axis, [(i, (i + by) % size) for i in range(size)])


def fetch_partners(load, slots, offset):
    half = load.shape[0] // 2
    ahead = passed_along(load[half:], "grp", -offset)
    behind = passed_along(load[:half], "grp", offset)
    return jnp.concatenate([ahead[slots[:half]], behind[slots[half:]]], 0)


def shards(query, key, value, out_grad, partner, tiles, tile_count):
    f32 = jnp.float32
    bf16 = jnp.bfloat16
    nodes, width = query.shape
    head_dim = width // HEADS
    scale = head_dim ** (-0.5)
    blocks_dev = nodes // BLOCK
    team = lax.axis_size("blk")
    cluster_blocks = blocks_dev * team
    keys_tile = TMAX * BLOCK
    heads4 = (blocks_dev, BLOCK, HEADS, head_dim)

    both = jnp.concatenate([key, value], 1)
    kv_cluster = lax.all_gather(both, "blk", axis=0, tiled=True)
    qg_cluster = lax.all_gather(jnp.concatenate([query, out_grad], 1), "blk", axis=0, tiled=True)
    partner_rows = jnp.stack(
        [fetch_partners(both, partner[step], step + 1) for step in range(ROUNDS)]
    )
    live = jnp.arange(TMAX, dtype=jnp.int32)[None, :] < tile_count[:, None]
    tile_live = jnp.broadcast_to(live[:, :, None], (blocks_dev, TMAX, BLOCK)).reshape(
        blocks_dev, keys_tile
    )

    kv_tiles = kv_cluster.reshape(cluster_blocks, BLOCK, 2 * width)[tiles].reshape(
        blocks_dev, keys_tile, 2 * width
    )
    k_tile = kv_tiles[..., :width].reshape(blocks_dev, keys_tile, HEADS, head_dim)
    v_tile = kv_tiles[..., width:].reshape(blocks_dev, keys_tile, HEADS, head_dim)
    pair_shape = (ROUNDS,) + heads4
    k_pair = partner_rows[..., :width].reshape(pair_shape)
    v_pair = partner_rows[..., width:].reshape(pair_shape)
    q4 = query.reshape(heads4)
    g4 = out_grad.reshape(heads4)

    s_loc = jnp.einsum("bqhd,bkhd->bhqk", q4, k_tile, preferred_element_type=f32) * scale
    s_loc = jnp.where(tile_live[:, None, None, :], s_loc, NEG_BIG)
    s_pair = jnp.einsum("bqhd,rbqhd->bhqr", q4, k_pair, preferred_element_type=f32) * scale
    top = jnp.maximum(jnp.max(s_loc, -1), jnp.max(s_pair, -1))
    e_loc = jnp.exp(s_loc - top[..., None])
    e_pair = jnp.exp(s_pair - top[..., None])
    total = jnp.sum(e_loc, -1) + jnp.sum(e_pair, -1)
    p_loc = e_loc / total[..., None]
    p_pair = e_pair / total[..., None]
    w_loc = p_loc.astype(bf16)
    w_pair = p_pair.astype(bf16)
    out_full = jnp.einsum("bhqk,bkhd->bqhd", w_loc, v_tile, preferred_element_type=f32)
    out_full = out_full + jnp.einsum("bhqr,rbqhd->bqhd", w_pair, v_pair, preferred_element_type=f32)
    delta = jnp.transpose(jnp.sum(g4.astype(f32) * out_full, -1), (0, 2, 1))
    d_loc = jnp.einsum("bqhd,bkhd->bhqk", g4, v_tile, preferred_element_type=f32)
    d_pair = jnp.einsum("bqhd,rbqhd->bhqr", g4, v_pair, preferred_element_type=f32)
    z_loc = (p_loc * (d_loc - delta[..., None])).astype(bf16)
    z_pair = (p_pair * (d_pair - delta[..., None])).astype(bf16)
    q_grad = jnp.einsum("bhqk,bkhd->bqhd", z_loc, k_tile, preferred_element_type=f32)
    q_grad = (
        q_grad + jnp.einsum("bhqr,rbqhd->bqhd", z_pair, k_pair, preferred_element_type=f32)
    ) * scale
    t_key = (
        jnp.einsum("bhqr,bqhd->rbqhd", z_pair, q4, preferred_element_type=f32) * scale
    ).astype(bf16)
    t_val = jnp.einsum("bhqr,bqhd->rbqhd", w_pair, g4, preferred_element_type=f32).astype(bf16)
    terms = jnp.concatenate(
        [t_key.reshape(ROUNDS, nodes, width), t_val.reshape(ROUNDS, nodes, width)], 2
    )
    returned = jnp.stack(
        [fetch_partners(terms[step], partner[step], step + 1) for step in range(ROUNDS)]
    )
    returned = jnp.sum(returned.astype(f32), 0)
    returned, qg_cluster = lax.optimization_barrier((returned, qg_cluster))

    stats = jnp.stack([top, total, delta], 1)
    stats = jnp.transpose(stats, (0, 3, 1, 2)).reshape(nodes, 3 * HEADS)
    stats = jnp.pad(stats, ((0, 0), (0, 128 - 3 * HEADS)))
    stats_cluster = lax.all_gather(stats, "blk", axis=0, tiled=True)[:, : 3 * HEADS]

    qg_tiles = qg_cluster.reshape(cluster_blocks, BLOCK, 2 * width)[tiles].reshape(
        blocks_dev, keys_tile, 2 * width
    )
    q_tile = qg_tiles[..., :width].reshape(blocks_dev, keys_tile, HEADS, head_dim)
    g_tile = qg_tiles[..., width:].reshape(blocks_dev, keys_tile, HEADS, head_dim)
    st = stats_cluster.reshape(cluster_blocks, BLOCK, 3, HEADS)[tiles].reshape(
        blocks_dev, keys_tile, 3, HEADS
    )
    st = jnp.transpose(st, (0, 2, 3, 1))
    top_t, total_t, delta_t = st[:, 0], st[:, 1], st[:, 2]
    k4 = key.reshape(heads4)
    v4 = value.reshape(heads4)
    s_key = jnp.einsum("bkhd,bqhd->bhkq", k4, q_tile, preferred_element_type=f32) * scale
    d_key = jnp.einsum("bkhd,bqhd->bhkq", v4, g_tile, preferred_element_type=f32)
    s_key, d_key = lax.optimization_barrier((s_key, d_key))
    s_key = jnp.where(tile_live[:, None, None, :], s_key, NEG_BIG)
    p_key = jnp.exp(s_key - top_t[:, :, None, :]) / total_t[:, :, None, :]
    w_key = p_key.astype(bf16)
    z_key = (p_key * (d_key - delta_t[:, :, None, :])).astype(bf16)
    k_sum = jnp.einsum("bhkq,bqhd->bkhd", z_key, q_tile, preferred_element_type=f32) * scale
    v_sum = jnp.einsum("bhkq,bqhd->bkhd", w_key, g_tile, preferred_element_type=f32)

    attended = out_full.reshape(nodes, width).astype(bf16)
    query_grad = q_grad.reshape(nodes, width).astype(bf16)
    key_grad = (k_sum.reshape(nodes, width) + returned[:, :width]).astype(bf16)
    value_grad = (v_sum.reshape(nodes, width) + returned[:, width:]).astype(bf16)
    return (attended, query_grad, key_grad, value_grad)


def solution(mesh):
    in_specs = (
        P(("grp", "blk"), None),
        P(("grp", "blk"), None),
        P(("grp", "blk"), None),
        P(("grp", "blk"), None),
        P(None, ("grp", "blk")),
        P(("grp", "blk"), None),
        P(("grp", "blk")),
    )
    out_specs = (
        P(("grp", "blk"), None),
        P(("grp", "blk"), None),
        P(("grp", "blk"), None),
        P(("grp", "blk"), None),
    )
    return jax.shard_map(shards, mesh=mesh, in_specs=in_specs, out_specs=out_specs, check_vma=False)
```

```python
import jax
import jax.numpy as jnp
from jax import lax
from jax.sharding import PartitionSpec as P

HEADS = 8
BLOCK = 128
TMAX = 6
ROUNDS = 2


NEG_BIG = -1e30


def passed_along(x, axis, by):
    size = lax.axis_size(axis)
    return lax.ppermute(x, axis, [(i, (i + by) % size) for i in range(size)])


def fetch_partners(load, slots, offset):
    half = load.shape[0] // 2
    ahead = passed_along(load[half:], "grp", -offset)
    behind = passed_along(load[:half], "grp", offset)
    return jnp.concatenate([ahead[slots[:half]], behind[slots[half:]]], 0)


def shards(query, key, value, out_grad, partner, tiles, tile_count):
    f32 = jnp.float32
    bf16 = jnp.bfloat16
    nodes, width = query.shape
    head_dim = width // HEADS
    scale = head_dim ** (-0.5)
    blocks_dev = nodes // BLOCK
    team = lax.axis_size("blk")
    cluster_blocks = blocks_dev * team
    keys_tile = TMAX * BLOCK
    heads4 = (blocks_dev, BLOCK, HEADS, head_dim)

    both = jnp.concatenate([key, value], 1)
    kv_cluster = lax.all_gather(both, "blk", axis=0, tiled=True)
    qg_cluster = lax.all_gather(jnp.concatenate([query, out_grad], 1), "blk", axis=0, tiled=True)
    partner_rows = jnp.stack(
        [fetch_partners(both, partner[step], step + 1) for step in range(ROUNDS)]
    )
    live = jnp.arange(TMAX, dtype=jnp.int32)[None, :] < tile_count[:, None]
    tile_live = jnp.broadcast_to(live[:, :, None], (blocks_dev, TMAX, BLOCK)).reshape(
        blocks_dev, keys_tile
    )

    kv_tiles = kv_cluster.reshape(cluster_blocks, BLOCK, 2 * width)[tiles].reshape(
        blocks_dev, keys_tile, 2 * width
    )
    k_tile = kv_tiles[..., :width].reshape(blocks_dev, keys_tile, HEADS, head_dim)
    v_tile = kv_tiles[..., width:].reshape(blocks_dev, keys_tile, HEADS, head_dim)
    pair_shape = (ROUNDS,) + heads4
    k_pair = partner_rows[..., :width].reshape(pair_shape)
    v_pair = partner_rows[..., width:].reshape(pair_shape)
    q4 = query.reshape(heads4)
    g4 = out_grad.reshape(heads4)

    s_loc = jnp.einsum("bqhd,bkhd->bhqk", q4, k_tile, preferred_element_type=f32) * scale
    s_loc = jnp.where(tile_live[:, None, None, :], s_loc, NEG_BIG)
    s_pair = jnp.einsum("bqhd,rbqhd->bhqr", q4, k_pair, preferred_element_type=f32) * scale
    top = jnp.maximum(jnp.max(s_loc, -1), jnp.max(s_pair, -1))
    e_loc = jnp.exp(s_loc - top[..., None])
    e_pair = jnp.exp(s_pair - top[..., None])
    total = jnp.sum(e_loc, -1) + jnp.sum(e_pair, -1)
    p_loc = e_loc / total[..., None]
    p_pair = e_pair / total[..., None]
    w_loc = p_loc.astype(bf16)
    w_pair = p_pair.astype(bf16)
    out_full = jnp.einsum("bhqk,bkhd->bqhd", w_loc, v_tile, preferred_element_type=f32)
    out_full = out_full + jnp.einsum("bhqr,rbqhd->bqhd", w_pair, v_pair, preferred_element_type=f32)
    delta = jnp.transpose(jnp.sum(g4.astype(f32) * out_full, -1), (0, 2, 1))
    d_loc = jnp.einsum("bqhd,bkhd->bhqk", g4, v_tile, preferred_element_type=f32)
    d_pair = jnp.einsum("bqhd,rbqhd->bhqr", g4, v_pair, preferred_element_type=f32)
    z_loc = (p_loc * (d_loc - delta[..., None])).astype(bf16)
    z_pair = (p_pair * (d_pair - delta[..., None])).astype(bf16)
    q_grad = jnp.einsum("bhqk,bkhd->bqhd", z_loc, k_tile, preferred_element_type=f32)
    q_grad = (
        q_grad + jnp.einsum("bhqr,rbqhd->bqhd", z_pair, k_pair, preferred_element_type=f32)
    ) * scale
    t_key = (
        jnp.einsum("bhqr,bqhd->rbqhd", z_pair, q4, preferred_element_type=f32) * scale
    ).astype(bf16)
    t_val = jnp.einsum("bhqr,bqhd->rbqhd", w_pair, g4, preferred_element_type=f32).astype(bf16)
    terms = jnp.concatenate(
        [t_key.reshape(ROUNDS, nodes, width), t_val.reshape(ROUNDS, nodes, width)], 2
    )
    returned = jnp.stack(
        [fetch_partners(terms[step], partner[step], step + 1) for step in range(ROUNDS)]
    )
    returned = jnp.sum(returned.astype(f32), 0)
    returned, qg_cluster = lax.optimization_barrier((returned, qg_cluster))

    stats = jnp.stack([top, total, delta], 1).reshape(blocks_dev * 3 * HEADS, BLOCK)
    rows = stats.shape[0]
    stats = jnp.pad(stats, ((0, nodes - rows), (0, 0)))
    stats_cluster = lax.all_gather(stats, "blk", axis=0, tiled=True)
    stats_cluster = stats_cluster.reshape(team, nodes, BLOCK)[:, :rows]

    qg_tiles = qg_cluster.reshape(cluster_blocks, BLOCK, 2 * width)[tiles].reshape(
        blocks_dev, keys_tile, 2 * width
    )
    q_tile = qg_tiles[..., :width].reshape(blocks_dev, keys_tile, HEADS, head_dim)
    g_tile = qg_tiles[..., width:].reshape(blocks_dev, keys_tile, HEADS, head_dim)
    st = stats_cluster.reshape(cluster_blocks, 3, HEADS, BLOCK)[tiles]
    st = jnp.transpose(st, (0, 2, 3, 1, 4)).reshape(blocks_dev, 3, HEADS, keys_tile)
    top_t, total_t, delta_t = st[:, 0], st[:, 1], st[:, 2]
    k4 = key.reshape(heads4)
    v4 = value.reshape(heads4)
    s_key = jnp.einsum("bkhd,bqhd->bhkq", k4, q_tile, preferred_element_type=f32) * scale
    d_key = jnp.einsum("bkhd,bqhd->bhkq", v4, g_tile, preferred_element_type=f32)
    s_key, d_key = lax.optimization_barrier((s_key, d_key))
    s_key = jnp.where(tile_live[:, None, None, :], s_key, NEG_BIG)
    p_key = jnp.exp(s_key - top_t[:, :, None, :]) / total_t[:, :, None, :]
    w_key = p_key.astype(bf16)
    z_key = (p_key * (d_key - delta_t[:, :, None, :])).astype(bf16)
    k_sum = jnp.einsum("bhkq,bqhd->bkhd", z_key, q_tile, preferred_element_type=f32) * scale
    v_sum = jnp.einsum("bhkq,bqhd->bkhd", w_key, g_tile, preferred_element_type=f32)

    attended = out_full.reshape(nodes, width).astype(bf16)
    query_grad = q_grad.reshape(nodes, width).astype(bf16)
    key_grad = (k_sum.reshape(nodes, width) + returned[:, :width]).astype(bf16)
    value_grad = (v_sum.reshape(nodes, width) + returned[:, width:]).astype(bf16)
    return (attended, query_grad, key_grad, value_grad)


def solution(mesh):
    in_specs = (
        P(("grp", "blk"), None),
        P(("grp", "blk"), None),
        P(("grp", "blk"), None),
        P(("grp", "blk"), None),
        P(None, ("grp", "blk")),
        P(("grp", "blk"), None),
        P(("grp", "blk")),
    )
    out_specs = (
        P(("grp", "blk"), None),
        P(("grp", "blk"), None),
        P(("grp", "blk"), None),
        P(("grp", "blk"), None),
    )
    return jax.shard_map(shards, mesh=mesh, in_specs=in_specs, out_specs=out_specs, check_vma=False)
```

```python
import jax
import jax.numpy as jnp
from jax import lax
from jax.sharding import PartitionSpec as P

HEADS = 8
BLOCK = 128
TMAX = 6
ROUNDS = 2


NEG_BIG = -1e30


def passed_along(x, axis, by):
    size = lax.axis_size(axis)
    return lax.ppermute(x, axis, [(i, (i + by) % size) for i in range(size)])


def fetch_partners(load, slots, offset):
    half = load.shape[0] // 2
    ahead = passed_along(load[half:], "grp", -offset)
    behind = passed_along(load[:half], "grp", offset)
    return jnp.concatenate([ahead[slots[:half]], behind[slots[half:]]], 0)


def shards(query, key, value, out_grad, partner, tiles, tile_count):
    f32 = jnp.float32
    bf16 = jnp.bfloat16
    nodes, width = query.shape
    head_dim = width // HEADS
    scale = head_dim ** (-0.5)
    blocks_dev = nodes // BLOCK
    team = lax.axis_size("blk")
    cluster_blocks = blocks_dev * team
    keys_tile = TMAX * BLOCK
    heads4 = (blocks_dev, BLOCK, HEADS, head_dim)

    both = jnp.concatenate([key, value], 1)
    kv_cluster = lax.all_gather(both, "blk", axis=0, tiled=True)
    qg_cluster = lax.all_gather(jnp.concatenate([query, out_grad], 1), "blk", axis=0, tiled=True)
    partner_rows = jnp.stack(
        [fetch_partners(both, partner[step], step + 1) for step in range(ROUNDS)]
    )
    live = jnp.arange(TMAX, dtype=jnp.int32)[None, :] < tile_count[:, None]
    tile_live = jnp.broadcast_to(live[:, :, None], (blocks_dev, TMAX, BLOCK)).reshape(
        blocks_dev, keys_tile
    )

    kv_tiles = kv_cluster.reshape(cluster_blocks, BLOCK, 2 * width)[tiles].reshape(
        blocks_dev, keys_tile, 2 * width
    )
    k_tile = kv_tiles[..., :width].reshape(blocks_dev, keys_tile, HEADS, head_dim)
    v_tile = kv_tiles[..., width:].reshape(blocks_dev, keys_tile, HEADS, head_dim)
    pair_shape = (ROUNDS,) + heads4
    k_pair = partner_rows[..., :width].reshape(pair_shape)
    v_pair = partner_rows[..., width:].reshape(pair_shape)
    q4 = query.reshape(heads4)
    g4 = out_grad.reshape(heads4)

    s_loc = jnp.einsum("bqhd,bkhd->bhqk", q4, k_tile, preferred_element_type=f32) * scale
    s_loc = jnp.where(tile_live[:, None, None, :], s_loc, NEG_BIG)
    s_pair = jnp.einsum("bqhd,rbqhd->bhqr", q4, k_pair, preferred_element_type=f32) * scale
    top = jnp.maximum(jnp.max(s_loc, -1), jnp.max(s_pair, -1))
    e_loc = jnp.exp(s_loc - top[..., None])
    e_pair = jnp.exp(s_pair - top[..., None])
    total = jnp.sum(e_loc, -1) + jnp.sum(e_pair, -1)
    p_loc = e_loc / total[..., None]
    p_pair = e_pair / total[..., None]
    w_loc = p_loc.astype(bf16)
    w_pair = p_pair.astype(bf16)
    out_full = jnp.einsum("bhqk,bkhd->bqhd", w_loc, v_tile, preferred_element_type=f32)
    out_full = out_full + jnp.einsum("bhqr,rbqhd->bqhd", w_pair, v_pair, preferred_element_type=f32)
    delta = jnp.transpose(jnp.sum(g4.astype(f32) * out_full, -1), (0, 2, 1))

    stats = jnp.stack([top, total, delta], 1).reshape(blocks_dev * 3 * HEADS, BLOCK)
    stats_cluster = lax.all_gather(stats, "blk", axis=0, tiled=True)
    stats_cluster, delta = lax.optimization_barrier((stats_cluster, delta))
    d_loc = jnp.einsum("bqhd,bkhd->bhqk", g4, v_tile, preferred_element_type=f32)
    d_pair = jnp.einsum("bqhd,rbqhd->bhqr", g4, v_pair, preferred_element_type=f32)
    z_loc = (p_loc * (d_loc - delta[..., None])).astype(bf16)
    z_pair = (p_pair * (d_pair - delta[..., None])).astype(bf16)
    q_grad = jnp.einsum("bhqk,bkhd->bqhd", z_loc, k_tile, preferred_element_type=f32)
    q_grad = (
        q_grad + jnp.einsum("bhqr,rbqhd->bqhd", z_pair, k_pair, preferred_element_type=f32)
    ) * scale
    t_key = (
        jnp.einsum("bhqr,bqhd->rbqhd", z_pair, q4, preferred_element_type=f32) * scale
    ).astype(bf16)
    t_val = jnp.einsum("bhqr,bqhd->rbqhd", w_pair, g4, preferred_element_type=f32).astype(bf16)
    terms = jnp.concatenate(
        [t_key.reshape(ROUNDS, nodes, width), t_val.reshape(ROUNDS, nodes, width)], 2
    )
    returned = jnp.stack(
        [fetch_partners(terms[step], partner[step], step + 1) for step in range(ROUNDS)]
    )
    returned = jnp.sum(returned.astype(f32), 0)
    returned, qg_cluster = lax.optimization_barrier((returned, qg_cluster))

    qg_tiles = qg_cluster.reshape(cluster_blocks, BLOCK, 2 * width)[tiles].reshape(
        blocks_dev, keys_tile, 2 * width
    )
    q_tile = qg_tiles[..., :width].reshape(blocks_dev, keys_tile, HEADS, head_dim)
    g_tile = qg_tiles[..., width:].reshape(blocks_dev, keys_tile, HEADS, head_dim)
    st = stats_cluster.reshape(cluster_blocks, 3, HEADS, BLOCK)[tiles]
    st = jnp.transpose(st, (0, 2, 3, 1, 4)).reshape(blocks_dev, 3, HEADS, keys_tile)
    top_t, total_t, delta_t = st[:, 0], st[:, 1], st[:, 2]
    k4 = key.reshape(heads4)
    v4 = value.reshape(heads4)
    s_key = jnp.einsum("bkhd,bqhd->bhkq", k4, q_tile, preferred_element_type=f32) * scale
    d_key = jnp.einsum("bkhd,bqhd->bhkq", v4, g_tile, preferred_element_type=f32)
    s_key = jnp.where(tile_live[:, None, None, :], s_key, NEG_BIG)
    p_key = jnp.exp(s_key - top_t[:, :, None, :]) / total_t[:, :, None, :]
    w_key = p_key.astype(bf16)
    z_key = (p_key * (d_key - delta_t[:, :, None, :])).astype(bf16)
    k_sum = jnp.einsum("bhkq,bqhd->bkhd", z_key, q_tile, preferred_element_type=f32) * scale
    v_sum = jnp.einsum("bhkq,bqhd->bkhd", w_key, g_tile, preferred_element_type=f32)

    attended = out_full.reshape(nodes, width).astype(bf16)
    query_grad = q_grad.reshape(nodes, width).astype(bf16)
    key_grad = (k_sum.reshape(nodes, width) + returned[:, :width]).astype(bf16)
    value_grad = (v_sum.reshape(nodes, width) + returned[:, width:]).astype(bf16)
    return (attended, query_grad, key_grad, value_grad)


def solution(mesh):
    in_specs = (
        P(("grp", "blk"), None),
        P(("grp", "blk"), None),
        P(("grp", "blk"), None),
        P(("grp", "blk"), None),
        P(None, ("grp", "blk")),
        P(("grp", "blk"), None),
        P(("grp", "blk")),
    )
    out_specs = (
        P(("grp", "blk"), None),
        P(("grp", "blk"), None),
        P(("grp", "blk"), None),
        P(("grp", "blk"), None),
    )
    return jax.shard_map(shards, mesh=mesh, in_specs=in_specs, out_specs=out_specs, check_vma=False)
```

```python
import functools

import jax
import jax.numpy as jnp
from jax import lax
from jax.experimental import pallas as pl
from jax.experimental.pallas import tpu as pltpu
from jax.sharding import PartitionSpec as P

HEADS = 8
BLOCK = 128
TMAX = 6
ROUNDS = 2


NEG_BIG = -1e30


def passed_along(x, axis, by):
    size = lax.axis_size(axis)
    return lax.ppermute(x, axis, [(i, (i + by) % size) for i in range(size)])


def fetch_partners(load, slots, offset):
    half = load.shape[0] // 2
    ahead = passed_along(load[half:], "grp", -offset)
    behind = passed_along(load[:half], "grp", offset)
    return jnp.concatenate([ahead[slots[:half]], behind[slots[half:]]], 0)


def key_side_kernel(count_ref, qg_ref, st_ref, k_ref, v_ref, ks_ref, vs_ref, *, scale):
    b = pl.program_id(0)
    width = k_ref.shape[-1]
    keys = qg_ref.shape[1]
    pair = 2 * (width // HEADS)
    half = pair // 2
    live = (lax.broadcasted_iota(jnp.int32, (1, keys), 1) // BLOCK) < count_ref[b]
    low = lax.broadcasted_iota(jnp.int32, (1, pair), 1) < half
    nt = (((1,), (1,)), ((), ()))
    for pr in range(width // pair):
        cols = pl.ds(pr * pair, pair)
        kp = k_ref[0, :, cols]
        vp = v_ref[0, :, cols]
        qp = qg_ref[0, :, cols]
        gp = qg_ref[0, :, pl.ds(width + pr * pair, pair)]
        zero = jnp.zeros_like(kp)
        k_out = []
        v_out = []
        for side in range(2):
            mine = low if side == 0 else jnp.logical_not(low)
            h = 2 * pr + side
            kh = jnp.where(mine, kp, zero)
            vh = jnp.where(mine, vp, zero)
            s = lax.dot_general(kh, qp, nt, preferred_element_type=jnp.float32) * scale
            d = lax.dot_general(vh, gp, nt, preferred_element_type=jnp.float32)
            top = st_ref[0, 0, pl.ds(h, 1), :]
            total = st_ref[0, 1, pl.ds(h, 1), :]
            delta = st_ref[0, 2, pl.ds(h, 1), :]
            p = jnp.where(live, jnp.exp(s - top) / total, 0.0)
            w = p.astype(jnp.bfloat16)
            z = (p * (d - delta)).astype(jnp.bfloat16)
            k_out.append(jnp.dot(z, qp, preferred_element_type=jnp.float32))
            v_out.append(jnp.dot(w, gp, preferred_element_type=jnp.float32))
        ks_ref[0, :, cols] = jnp.where(low, k_out[0], k_out[1]) * scale
        vs_ref[0, :, cols] = jnp.where(low, v_out[0], v_out[1])


def key_side(tile_count, qg_tiles, st, k3, v3, scale):
    blocks, keys, width2 = qg_tiles.shape
    width = width2 // 2
    grid_spec = pltpu.PrefetchScalarGridSpec(
        num_scalar_prefetch=1,
        grid=(blocks,),
        in_specs=[
            pl.BlockSpec((1, keys, width2), lambda b, c: (b, 0, 0)),
            pl.BlockSpec((1, 3, HEADS, keys), lambda b, c: (b, 0, 0, 0)),
            pl.BlockSpec((1, BLOCK, width), lambda b, c: (b, 0, 0)),
            pl.BlockSpec((1, BLOCK, width), lambda b, c: (b, 0, 0)),
        ],
        out_specs=[
            pl.BlockSpec((1, BLOCK, width), lambda b, c: (b, 0, 0)),
            pl.BlockSpec((1, BLOCK, width), lambda b, c: (b, 0, 0)),
        ],
    )
    flops = blocks * (width // 128) * 2 * 4 * 2 * BLOCK * 128 * keys
    cost = pl.CostEstimate(flops=flops, transcendentals=blocks * HEADS * BLOCK * keys,
                           bytes_accessed=qg_tiles.size * 2 + st.size * 4 + 6 * blocks * BLOCK * width * 4)
    return pl.pallas_call(
        functools.partial(key_side_kernel, scale=scale),
        grid_spec=grid_spec,
        out_shape=[jax.ShapeDtypeStruct((blocks, BLOCK, width), jnp.float32)] * 2,
        cost_estimate=cost,
    )(tile_count, qg_tiles, st, k3, v3)


def shards(query, key, value, out_grad, partner, tiles, tile_count):
    f32 = jnp.float32
    bf16 = jnp.bfloat16
    nodes, width = query.shape
    head_dim = width // HEADS
    scale = head_dim ** (-0.5)
    blocks_dev = nodes // BLOCK
    team = lax.axis_size("blk")
    cluster_blocks = blocks_dev * team
    keys_tile = TMAX * BLOCK
    heads4 = (blocks_dev, BLOCK, HEADS, head_dim)

    both = jnp.concatenate([key, value], 1)
    kv_cluster = lax.all_gather(both, "blk", axis=0, tiled=True)
    qg_cluster = lax.all_gather(jnp.concatenate([query, out_grad], 1), "blk", axis=0, tiled=True)
    partner_rows = jnp.stack(
        [fetch_partners(both, partner[step], step + 1) for step in range(ROUNDS)]
    )
    live = jnp.arange(TMAX, dtype=jnp.int32)[None, :] < tile_count[:, None]
    tile_live = jnp.broadcast_to(live[:, :, None], (blocks_dev, TMAX, BLOCK)).reshape(
        blocks_dev, keys_tile
    )

    kv_tiles = kv_cluster.reshape(cluster_blocks, BLOCK, 2 * width)[tiles].reshape(
        blocks_dev, keys_tile, 2 * width
    )
    k_tile = kv_tiles[..., :width].reshape(blocks_dev, keys_tile, HEADS, head_dim)
    v_tile = kv_tiles[..., width:].reshape(blocks_dev, keys_tile, HEADS, head_dim)
    pair_shape = (ROUNDS,) + heads4
    k_pair = partner_rows[..., :width].reshape(pair_shape)
    v_pair = partner_rows[..., width:].reshape(pair_shape)
    q4 = query.reshape(heads4)
    g4 = out_grad.reshape(heads4)

    s_loc = jnp.einsum("bqhd,bkhd->bhqk", q4, k_tile, preferred_element_type=f32) * scale
    s_loc = jnp.where(tile_live[:, None, None, :], s_loc, NEG_BIG)
    s_pair = jnp.einsum("bqhd,rbqhd->bhqr", q4, k_pair, preferred_element_type=f32) * scale
    top = jnp.maximum(jnp.max(s_loc, -1), jnp.max(s_pair, -1))
    e_loc = jnp.exp(s_loc - top[..., None])
    e_pair = jnp.exp(s_pair - top[..., None])
    total = jnp.sum(e_loc, -1) + jnp.sum(e_pair, -1)
    p_loc = e_loc / total[..., None]
    p_pair = e_pair / total[..., None]
    w_loc = p_loc.astype(bf16)
    w_pair = p_pair.astype(bf16)
    out_full = jnp.einsum("bhqk,bkhd->bqhd", w_loc, v_tile, preferred_element_type=f32)
    out_full = out_full + jnp.einsum("bhqr,rbqhd->bqhd", w_pair, v_pair, preferred_element_type=f32)
    delta = jnp.transpose(jnp.sum(g4.astype(f32) * out_full, -1), (0, 2, 1))

    stats = jnp.stack([top, total, delta], 1).reshape(blocks_dev * 3 * HEADS, BLOCK)
    stats_cluster = lax.all_gather(stats, "blk", axis=0, tiled=True)
    stats_cluster, delta = lax.optimization_barrier((stats_cluster, delta))
    d_loc = jnp.einsum("bqhd,bkhd->bhqk", g4, v_tile, preferred_element_type=f32)
    d_pair = jnp.einsum("bqhd,rbqhd->bhqr", g4, v_pair, preferred_element_type=f32)
    z_loc = (p_loc * (d_loc - delta[..., None])).astype(bf16)
    z_pair = (p_pair * (d_pair - delta[..., None])).astype(bf16)
    q_grad = jnp.einsum("bhqk,bkhd->bqhd", z_loc, k_tile, preferred_element_type=f32)
    q_grad = (
        q_grad + jnp.einsum("bhqr,rbqhd->bqhd", z_pair, k_pair, preferred_element_type=f32)
    ) * scale
    t_key = (
        jnp.einsum("bhqr,bqhd->rbqhd", z_pair, q4, preferred_element_type=f32) * scale
    ).astype(bf16)
    t_val = jnp.einsum("bhqr,bqhd->rbqhd", w_pair, g4, preferred_element_type=f32).astype(bf16)
    terms = jnp.concatenate(
        [t_key.reshape(ROUNDS, nodes, width), t_val.reshape(ROUNDS, nodes, width)], 2
    )
    returned = jnp.stack(
        [fetch_partners(terms[step], partner[step], step + 1) for step in range(ROUNDS)]
    )
    returned = jnp.sum(returned.astype(f32), 0)
    returned, qg_cluster = lax.optimization_barrier((returned, qg_cluster))

    qg_tiles = qg_cluster.reshape(cluster_blocks, BLOCK, 2 * width)[tiles].reshape(
        blocks_dev, keys_tile, 2 * width
    )
    st = stats_cluster.reshape(cluster_blocks, 3, HEADS, BLOCK)[tiles]
    st = jnp.transpose(st, (0, 2, 3, 1, 4)).reshape(blocks_dev, 3, HEADS, keys_tile)
    k_sum, v_sum = key_side(
        tile_count,
        qg_tiles,
        st,
        key.reshape(blocks_dev, BLOCK, width),
        value.reshape(blocks_dev, BLOCK, width),
        scale,
    )

    attended = out_full.reshape(nodes, width).astype(bf16)
    query_grad = q_grad.reshape(nodes, width).astype(bf16)
    key_grad = (k_sum.reshape(nodes, width) + returned[:, :width]).astype(bf16)
    value_grad = (v_sum.reshape(nodes, width) + returned[:, width:]).astype(bf16)
    return (attended, query_grad, key_grad, value_grad)


def solution(mesh):
    in_specs = (
        P(("grp", "blk"), None),
        P(("grp", "blk"), None),
        P(("grp", "blk"), None),
        P(("grp", "blk"), None),
        P(None, ("grp", "blk")),
        P(("grp", "blk"), None),
        P(("grp", "blk")),
    )
    out_specs = (
        P(("grp", "blk"), None),
        P(("grp", "blk"), None),
        P(("grp", "blk"), None),
        P(("grp", "blk"), None),
    )
    return jax.shard_map(shards, mesh=mesh, in_specs=in_specs, out_specs=out_specs, check_vma=False)
```

```python
import functools

import jax
import jax.numpy as jnp
from jax import lax
from jax.experimental import pallas as pl
from jax.experimental.pallas import tpu as pltpu
from jax.sharding import PartitionSpec as P

HEADS = 8
BLOCK = 128
TMAX = 6
ROUNDS = 2


NEG_BIG = -1e30


def passed_along(x, axis, by):
    size = lax.axis_size(axis)
    return lax.ppermute(x, axis, [(i, (i + by) % size) for i in range(size)])


def fetch_partners(load, slots, offset):
    half = load.shape[0] // 2
    ahead = passed_along(load[half:], "grp", -offset)
    behind = passed_along(load[:half], "grp", offset)
    return jnp.concatenate([ahead[slots[:half]], behind[slots[half:]]], 0)


def query_side_kernel(count_ref, kv_ref, q_ref, g_ref, pair_ref, out_ref, qgrad_ref, term_ref, st_ref, *, scale):
    b = pl.program_id(0)
    width = q_ref.shape[-1]
    keys = kv_ref.shape[1]
    pair = 2 * (width // HEADS)
    half = pair // 2
    f32, bf16 = jnp.float32, jnp.bfloat16
    live = (lax.broadcasted_iota(jnp.int32, (1, keys), 1) // BLOCK) < count_ref[b]
    low = lax.broadcasted_iota(jnp.int32, (1, pair), 1) < half
    lane = lax.broadcasted_iota(jnp.int32, (1, pair), 1)
    nt = (((1,), (1,)), ((), ()))
    stats = jnp.zeros((BLOCK, pair), f32)
    for pr in range(width // pair):
        cols = pl.ds(pr * pair, pair)
        qp = q_ref[0, :, cols]
        gp = g_ref[0, :, cols]
        kp = kv_ref[0, :, cols]
        vp = kv_ref[0, :, pl.ds(width + pr * pair, pair)]
        kr = [pair_ref[r, 0, :, cols].astype(f32) for r in range(ROUNDS)]
        vr = [pair_ref[r, 0, :, pl.ds(width + pr * pair, pair)].astype(f32) for r in range(ROUNDS)]
        qf = qp.astype(f32)
        gf = gp.astype(f32)
        outs, grads = [], []
        tk = [[] for _ in range(ROUNDS)]
        tv = [[] for _ in range(ROUNDS)]
        for side in range(2):
            mine = low if side == 0 else jnp.logical_not(low)
            h = 2 * pr + side
            qh = jnp.where(mine, qp, jnp.zeros_like(qp))
            gh = jnp.where(mine, gp, jnp.zeros_like(gp))
            qhf = jnp.where(mine, qf, 0.0)
            ghf = jnp.where(mine, gf, 0.0)
            s_loc = lax.dot_general(qh, kp, nt, preferred_element_type=f32) * scale
            s_loc = jnp.where(live, s_loc, NEG_BIG)
            s_pair = [jnp.sum(qhf * kr[r], -1, keepdims=True) * scale for r in range(ROUNDS)]
            top = jnp.max(s_loc, -1, keepdims=True)
            for r in range(ROUNDS):
                top = jnp.maximum(top, s_pair[r])
            e_loc = jnp.exp(s_loc - top)
            e_pair = [jnp.exp(s_pair[r] - top) for r in range(ROUNDS)]
            total = jnp.sum(e_loc, -1, keepdims=True)
            for r in range(ROUNDS):
                total = total + e_pair[r]
            p_loc = e_loc / total
            p_pair = [e_pair[r] / total for r in range(ROUNDS)]
            w_loc = p_loc.astype(bf16)
            w_pair = [p_pair[r].astype(bf16).astype(f32) for r in range(ROUNDS)]
            out = jnp.dot(w_loc, vp, preferred_element_type=f32)
            for r in range(ROUNDS):
                out = out + w_pair[r] * vr[r]
            delta = jnp.sum(jnp.where(mine, gf * out, 0.0), -1, keepdims=True)
            d_loc = lax.dot_general(gh, vp, nt, preferred_element_type=f32)
            d_pair = [jnp.sum(ghf * vr[r], -1, keepdims=True) for r in range(ROUNDS)]
            z_loc = (p_loc * (d_loc - delta)).astype(bf16)
            z_pair = [(p_pair[r] * (d_pair[r] - delta)).astype(bf16).astype(f32) for r in range(ROUNDS)]
            grad = jnp.dot(z_loc, kp, preferred_element_type=f32)
            for r in range(ROUNDS):
                grad = grad + z_pair[r] * kr[r]
            outs.append(out)
            grads.append(grad * scale)
            for r in range(ROUNDS):
                tk[r].append(z_pair[r] * qf * scale)
                tv[r].append(w_pair[r] * gf)
            for i, value in enumerate((top, total, delta)):
                stats = jnp.where(lane == i * HEADS + h, value, stats)
        out_ref[0, :, cols] = jnp.where(low, outs[0], outs[1])
        qgrad_ref[0, :, cols] = jnp.where(low, grads[0], grads[1]).astype(bf16)
        for r in range(ROUNDS):
            term_ref[r, 0, :, cols] = jnp.where(low, tk[r][0], tk[r][1]).astype(bf16)
            term_ref[r, 0, :, pl.ds(width + pr * pair, pair)] = jnp.where(low, tv[r][0], tv[r][1]).astype(bf16)
    st_ref[0] = stats


def query_side(tile_count, kv_tiles, q3, g3, pair_rows, scale):
    blocks, keys, width2 = kv_tiles.shape
    width = width2 // 2
    grid_spec = pltpu.PrefetchScalarGridSpec(
        num_scalar_prefetch=1,
        grid=(blocks,),
        in_specs=[
            pl.BlockSpec((1, keys, width2), lambda b, c: (b, 0, 0)),
            pl.BlockSpec((1, BLOCK, width), lambda b, c: (b, 0, 0)),
            pl.BlockSpec((1, BLOCK, width), lambda b, c: (b, 0, 0)),
            pl.BlockSpec((ROUNDS, 1, BLOCK, width2), lambda b, c: (0, b, 0, 0)),
        ],
        out_specs=[
            pl.BlockSpec((1, BLOCK, width), lambda b, c: (b, 0, 0)),
            pl.BlockSpec((1, BLOCK, width), lambda b, c: (b, 0, 0)),
            pl.BlockSpec((ROUNDS, 1, BLOCK, width2), lambda b, c: (0, b, 0, 0)),
            pl.BlockSpec((1, BLOCK, 2 * (width // HEADS)), lambda b, c: (b, 0, 0)),
        ],
    )
    flops = blocks * (width // 128) * 2 * 4 * 2 * BLOCK * 128 * keys
    cost = pl.CostEstimate(flops=flops, transcendentals=blocks * HEADS * BLOCK * keys,
                           bytes_accessed=kv_tiles.size * 2 + pair_rows.size * 2 + 8 * blocks * BLOCK * width * 4)
    return pl.pallas_call(
        functools.partial(query_side_kernel, scale=scale),
        grid_spec=grid_spec,
        out_shape=[
            jax.ShapeDtypeStruct((blocks, BLOCK, width), jnp.float32),
            jax.ShapeDtypeStruct((blocks, BLOCK, width), jnp.bfloat16),
            jax.ShapeDtypeStruct((ROUNDS, blocks, BLOCK, width2), jnp.bfloat16),
            jax.ShapeDtypeStruct((blocks, BLOCK, 2 * (width // HEADS)), jnp.float32),
        ],
        cost_estimate=cost,
    )(tile_count, kv_tiles, q3, g3, pair_rows)


def key_side_kernel(count_ref, qg_ref, st_ref, k_ref, v_ref, ks_ref, vs_ref, *, scale):
    b = pl.program_id(0)
    width = k_ref.shape[-1]
    keys = qg_ref.shape[1]
    pair = 2 * (width // HEADS)
    half = pair // 2
    live = (lax.broadcasted_iota(jnp.int32, (1, keys), 1) // BLOCK) < count_ref[b]
    low = lax.broadcasted_iota(jnp.int32, (1, pair), 1) < half
    nt = (((1,), (1,)), ((), ()))
    for pr in range(width // pair):
        cols = pl.ds(pr * pair, pair)
        kp = k_ref[0, :, cols]
        vp = v_ref[0, :, cols]
        qp = qg_ref[0, :, cols]
        gp = qg_ref[0, :, pl.ds(width + pr * pair, pair)]
        zero = jnp.zeros_like(kp)
        k_out = []
        v_out = []
        for side in range(2):
            mine = low if side == 0 else jnp.logical_not(low)
            h = 2 * pr + side
            kh = jnp.where(mine, kp, zero)
            vh = jnp.where(mine, vp, zero)
            s = lax.dot_general(kh, qp, nt, preferred_element_type=jnp.float32) * scale
            d = lax.dot_general(vh, gp, nt, preferred_element_type=jnp.float32)
            top = st_ref[0, 0, pl.ds(h, 1), :]
            total = st_ref[0, 1, pl.ds(h, 1), :]
            delta = st_ref[0, 2, pl.ds(h, 1), :]
            p = jnp.where(live, jnp.exp(s - top) / total, 0.0)
            w = p.astype(jnp.bfloat16)
            z = (p * (d - delta)).astype(jnp.bfloat16)
            k_out.append(jnp.dot(z, qp, preferred_element_type=jnp.float32))
            v_out.append(jnp.dot(w, gp, preferred_element_type=jnp.float32))
        ks_ref[0, :, cols] = jnp.where(low, k_out[0], k_out[1]) * scale
        vs_ref[0, :, cols] = jnp.where(low, v_out[0], v_out[1])


def key_side(tile_count, qg_tiles, st, k3, v3, scale):
    blocks, keys, width2 = qg_tiles.shape
    width = width2 // 2
    grid_spec = pltpu.PrefetchScalarGridSpec(
        num_scalar_prefetch=1,
        grid=(blocks,),
        in_specs=[
            pl.BlockSpec((1, keys, width2), lambda b, c: (b, 0, 0)),
            pl.BlockSpec((1, 3, HEADS, keys), lambda b, c: (b, 0, 0, 0)),
            pl.BlockSpec((1, BLOCK, width), lambda b, c: (b, 0, 0)),
            pl.BlockSpec((1, BLOCK, width), lambda b, c: (b, 0, 0)),
        ],
        out_specs=[
            pl.BlockSpec((1, BLOCK, width), lambda b, c: (b, 0, 0)),
            pl.BlockSpec((1, BLOCK, width), lambda b, c: (b, 0, 0)),
        ],
    )
    flops = blocks * (width // 128) * 2 * 4 * 2 * BLOCK * 128 * keys
    cost = pl.CostEstimate(flops=flops, transcendentals=blocks * HEADS * BLOCK * keys,
                           bytes_accessed=qg_tiles.size * 2 + st.size * 4 + 6 * blocks * BLOCK * width * 4)
    return pl.pallas_call(
        functools.partial(key_side_kernel, scale=scale),
        grid_spec=grid_spec,
        out_shape=[jax.ShapeDtypeStruct((blocks, BLOCK, width), jnp.float32)] * 2,
        cost_estimate=cost,
    )(tile_count, qg_tiles, st, k3, v3)


def shards(query, key, value, out_grad, partner, tiles, tile_count):
    f32 = jnp.float32
    bf16 = jnp.bfloat16
    nodes, width = query.shape
    head_dim = width // HEADS
    scale = head_dim ** (-0.5)
    blocks_dev = nodes // BLOCK
    team = lax.axis_size("blk")
    cluster_blocks = blocks_dev * team
    keys_tile = TMAX * BLOCK

    both = jnp.concatenate([key, value], 1)
    kv_cluster = lax.all_gather(both, "blk", axis=0, tiled=True)
    qg_cluster = lax.all_gather(jnp.concatenate([query, out_grad], 1), "blk", axis=0, tiled=True)
    partner_rows = jnp.stack(
        [fetch_partners(both, partner[step], step + 1) for step in range(ROUNDS)]
    )

    kv_tiles = kv_cluster.reshape(cluster_blocks, BLOCK, 2 * width)[tiles].reshape(
        blocks_dev, keys_tile, 2 * width
    )
    out_full, query_grad, terms, stats = query_side(
        tile_count,
        kv_tiles,
        query.reshape(blocks_dev, BLOCK, width),
        out_grad.reshape(blocks_dev, BLOCK, width),
        partner_rows.reshape(ROUNDS, blocks_dev, BLOCK, 2 * width),
        scale,
    )

    stats = stats[..., : 3 * HEADS].reshape(blocks_dev, BLOCK, 3, HEADS)
    stats = jnp.transpose(stats, (0, 2, 3, 1)).reshape(blocks_dev * 3 * HEADS, BLOCK)
    stats_cluster = lax.all_gather(stats, "blk", axis=0, tiled=True)

    terms = terms.reshape(ROUNDS, nodes, 2 * width)
    returned = jnp.stack(
        [fetch_partners(terms[step], partner[step], step + 1) for step in range(ROUNDS)]
    )
    returned = jnp.sum(returned.astype(f32), 0)
    returned, stats_cluster, qg_cluster = lax.optimization_barrier(
        (returned, stats_cluster, qg_cluster)
    )

    qg_tiles = qg_cluster.reshape(cluster_blocks, BLOCK, 2 * width)[tiles].reshape(
        blocks_dev, keys_tile, 2 * width
    )
    st = stats_cluster.reshape(cluster_blocks, 3, HEADS, BLOCK)[tiles]
    st = jnp.transpose(st, (0, 2, 3, 1, 4)).reshape(blocks_dev, 3, HEADS, keys_tile)
    k_sum, v_sum = key_side(
        tile_count,
        qg_tiles,
        st,
        key.reshape(blocks_dev, BLOCK, width),
        value.reshape(blocks_dev, BLOCK, width),
        scale,
    )

    attended = out_full.reshape(nodes, width).astype(bf16)
    query_grad = query_grad.reshape(nodes, width)
    key_grad = (k_sum.reshape(nodes, width) + returned[:, :width]).astype(bf16)
    value_grad = (v_sum.reshape(nodes, width) + returned[:, width:]).astype(bf16)
    return (attended, query_grad, key_grad, value_grad)


def solution(mesh):
    in_specs = (
        P(("grp", "blk"), None),
        P(("grp", "blk"), None),
        P(("grp", "blk"), None),
        P(("grp", "blk"), None),
        P(None, ("grp", "blk")),
        P(("grp", "blk"), None),
        P(("grp", "blk")),
    )
    out_specs = (
        P(("grp", "blk"), None),
        P(("grp", "blk"), None),
        P(("grp", "blk"), None),
        P(("grp", "blk"), None),
    )
    return jax.shard_map(shards, mesh=mesh, in_specs=in_specs, out_specs=out_specs, check_vma=False)
```

```python
import functools

import jax
import jax.numpy as jnp
from jax import lax
from jax.experimental import pallas as pl
from jax.experimental.pallas import tpu as pltpu
from jax.sharding import PartitionSpec as P

HEADS = 8
BLOCK = 128
TMAX = 6
ROUNDS = 2


NEG_BIG = -1e30


def passed_along(x, axis, by):
    size = lax.axis_size(axis)
    return lax.ppermute(x, axis, [(i, (i + by) % size) for i in range(size)])


def fetch_partners(load, slots, offset):
    half = load.shape[0] // 2
    ahead = passed_along(load[half:], "grp", -offset)
    behind = passed_along(load[:half], "grp", offset)
    return jnp.concatenate([ahead[slots[:half]], behind[slots[half:]]], 0)


def query_side_kernel(
    count_ref, tiles_ref, kv_ref, q_ref, g_ref, pair_ref, out_ref, qgrad_ref, term_ref, st_ref, *, scale
):
    b = pl.program_id(0)
    width = q_ref.shape[-1]
    slots = tiles_ref.shape[1]
    keys = slots * BLOCK
    ids = [tiles_ref[b, t] for t in range(slots)]
    pair = 2 * (width // HEADS)
    half = pair // 2
    f32, bf16 = jnp.float32, jnp.bfloat16
    live = (lax.broadcasted_iota(jnp.int32, (1, keys), 1) // BLOCK) < count_ref[b]
    low = lax.broadcasted_iota(jnp.int32, (1, pair), 1) < half
    lane = lax.broadcasted_iota(jnp.int32, (1, pair), 1)
    nt = (((1,), (1,)), ((), ()))
    stats = jnp.zeros((BLOCK, pair), f32)
    for pr in range(width // pair):
        cols = pl.ds(pr * pair, pair)
        qp = q_ref[0, :, cols]
        gp = g_ref[0, :, cols]
        kp = jnp.concatenate([kv_ref[i, :, cols] for i in ids], 0)
        vp = jnp.concatenate([kv_ref[i, :, pl.ds(width + pr * pair, pair)] for i in ids], 0)
        kr = [pair_ref[r, 0, :, cols].astype(f32) for r in range(ROUNDS)]
        vr = [pair_ref[r, 0, :, pl.ds(width + pr * pair, pair)].astype(f32) for r in range(ROUNDS)]
        qf = qp.astype(f32)
        gf = gp.astype(f32)
        outs, grads = [], []
        tk = [[] for _ in range(ROUNDS)]
        tv = [[] for _ in range(ROUNDS)]
        for side in range(2):
            mine = low if side == 0 else jnp.logical_not(low)
            h = 2 * pr + side
            qh = jnp.where(mine, qp, jnp.zeros_like(qp))
            gh = jnp.where(mine, gp, jnp.zeros_like(gp))
            qhf = jnp.where(mine, qf, 0.0)
            ghf = jnp.where(mine, gf, 0.0)
            s_loc = lax.dot_general(qh, kp, nt, preferred_element_type=f32) * scale
            s_loc = jnp.where(live, s_loc, NEG_BIG)
            s_pair = [jnp.sum(qhf * kr[r], -1, keepdims=True) * scale for r in range(ROUNDS)]
            top = jnp.max(s_loc, -1, keepdims=True)
            for r in range(ROUNDS):
                top = jnp.maximum(top, s_pair[r])
            e_loc = jnp.exp(s_loc - top)
            e_pair = [jnp.exp(s_pair[r] - top) for r in range(ROUNDS)]
            total = jnp.sum(e_loc, -1, keepdims=True)
            for r in range(ROUNDS):
                total = total + e_pair[r]
            p_loc = e_loc / total
            p_pair = [e_pair[r] / total for r in range(ROUNDS)]
            w_loc = p_loc.astype(bf16)
            w_pair = [p_pair[r].astype(bf16).astype(f32) for r in range(ROUNDS)]
            out = jnp.dot(w_loc, vp, preferred_element_type=f32)
            for r in range(ROUNDS):
                out = out + w_pair[r] * vr[r]
            delta = jnp.sum(jnp.where(mine, gf * out, 0.0), -1, keepdims=True)
            d_loc = lax.dot_general(gh, vp, nt, preferred_element_type=f32)
            d_pair = [jnp.sum(ghf * vr[r], -1, keepdims=True) for r in range(ROUNDS)]
            z_loc = (p_loc * (d_loc - delta)).astype(bf16)
            z_pair = [(p_pair[r] * (d_pair[r] - delta)).astype(bf16).astype(f32) for r in range(ROUNDS)]
            grad = jnp.dot(z_loc, kp, preferred_element_type=f32)
            for r in range(ROUNDS):
                grad = grad + z_pair[r] * kr[r]
            outs.append(out)
            grads.append(grad * scale)
            for r in range(ROUNDS):
                tk[r].append(z_pair[r] * qf * scale)
                tv[r].append(w_pair[r] * gf)
            for i, value in enumerate((top, total, delta)):
                stats = jnp.where(lane == i * HEADS + h, value, stats)
        out_ref[0, :, cols] = jnp.where(low, outs[0], outs[1])
        qgrad_ref[0, :, cols] = jnp.where(low, grads[0], grads[1]).astype(bf16)
        for r in range(ROUNDS):
            term_ref[r, 0, :, cols] = jnp.where(low, tk[r][0], tk[r][1]).astype(bf16)
            term_ref[r, 0, :, pl.ds(width + pr * pair, pair)] = jnp.where(low, tv[r][0], tv[r][1]).astype(bf16)
    st_ref[0] = stats


def query_side(tile_count, tiles, kv_blocks, q3, g3, pair_rows, scale):
    blocks, slots = tiles.shape
    keys = slots * BLOCK
    width2 = kv_blocks.shape[-1]
    width = width2 // 2
    grid_spec = pltpu.PrefetchScalarGridSpec(
        num_scalar_prefetch=2,
        grid=(blocks,),
        in_specs=[
            pl.BlockSpec(memory_space=pltpu.VMEM),
            pl.BlockSpec((1, BLOCK, width), lambda b, c, t: (b, 0, 0)),
            pl.BlockSpec((1, BLOCK, width), lambda b, c, t: (b, 0, 0)),
            pl.BlockSpec((ROUNDS, 1, BLOCK, width2), lambda b, c, t: (0, b, 0, 0)),
        ],
        out_specs=[
            pl.BlockSpec((1, BLOCK, width), lambda b, c, t: (b, 0, 0)),
            pl.BlockSpec((1, BLOCK, width), lambda b, c, t: (b, 0, 0)),
            pl.BlockSpec((ROUNDS, 1, BLOCK, width2), lambda b, c, t: (0, b, 0, 0)),
            pl.BlockSpec((1, BLOCK, 2 * (width // HEADS)), lambda b, c, t: (b, 0, 0)),
        ],
    )
    flops = blocks * (width // 128) * 2 * 4 * 2 * BLOCK * 128 * keys
    cost = pl.CostEstimate(flops=flops, transcendentals=blocks * HEADS * BLOCK * keys,
                           bytes_accessed=kv_blocks.size * 2 + pair_rows.size * 2 + 8 * blocks * BLOCK * width * 4)
    return pl.pallas_call(
        functools.partial(query_side_kernel, scale=scale),
        grid_spec=grid_spec,
        out_shape=[
            jax.ShapeDtypeStruct((blocks, BLOCK, width), jnp.float32),
            jax.ShapeDtypeStruct((blocks, BLOCK, width), jnp.bfloat16),
            jax.ShapeDtypeStruct((ROUNDS, blocks, BLOCK, width2), jnp.bfloat16),
            jax.ShapeDtypeStruct((blocks, BLOCK, 2 * (width // HEADS)), jnp.float32),
        ],
        cost_estimate=cost,
    )(tile_count, tiles, kv_blocks, q3, g3, pair_rows)


def key_side_kernel(count_ref, tiles_ref, qg_ref, st_ref, k_ref, v_ref, ks_ref, vs_ref, *, scale):
    b = pl.program_id(0)
    width = k_ref.shape[-1]
    slots = tiles_ref.shape[1]
    keys = slots * BLOCK
    ids = [tiles_ref[b, t] for t in range(slots)]
    pair = 2 * (width // HEADS)
    half = pair // 2
    live = (lax.broadcasted_iota(jnp.int32, (1, keys), 1) // BLOCK) < count_ref[b]
    low = lax.broadcasted_iota(jnp.int32, (1, pair), 1) < half
    nt = (((1,), (1,)), ((), ()))
    for pr in range(width // pair):
        cols = pl.ds(pr * pair, pair)
        kp = k_ref[0, :, cols]
        vp = v_ref[0, :, cols]
        qp = jnp.concatenate([qg_ref[i, :, cols] for i in ids], 0)
        gp = jnp.concatenate([qg_ref[i, :, pl.ds(width + pr * pair, pair)] for i in ids], 0)
        zero = jnp.zeros_like(kp)
        k_out = []
        v_out = []
        for side in range(2):
            mine = low if side == 0 else jnp.logical_not(low)
            h = 2 * pr + side
            kh = jnp.where(mine, kp, zero)
            vh = jnp.where(mine, vp, zero)
            s = lax.dot_general(kh, qp, nt, preferred_element_type=jnp.float32) * scale
            d = lax.dot_general(vh, gp, nt, preferred_element_type=jnp.float32)
            top, total, delta = [
                jnp.concatenate([st_ref[i, j, pl.ds(h, 1), :] for i in ids], 1) for j in range(3)
            ]
            p = jnp.where(live, jnp.exp(s - top) / total, 0.0)
            w = p.astype(jnp.bfloat16)
            z = (p * (d - delta)).astype(jnp.bfloat16)
            k_out.append(jnp.dot(z, qp, preferred_element_type=jnp.float32))
            v_out.append(jnp.dot(w, gp, preferred_element_type=jnp.float32))
        ks_ref[0, :, cols] = jnp.where(low, k_out[0], k_out[1]) * scale
        vs_ref[0, :, cols] = jnp.where(low, v_out[0], v_out[1])


def key_side(tile_count, tiles, qg_blocks, st, k3, v3, scale):
    blocks, slots = tiles.shape
    keys = slots * BLOCK
    width = k3.shape[-1]
    grid_spec = pltpu.PrefetchScalarGridSpec(
        num_scalar_prefetch=2,
        grid=(blocks,),
        in_specs=[
            pl.BlockSpec(memory_space=pltpu.VMEM),
            pl.BlockSpec(memory_space=pltpu.VMEM),
            pl.BlockSpec((1, BLOCK, width), lambda b, c, t: (b, 0, 0)),
            pl.BlockSpec((1, BLOCK, width), lambda b, c, t: (b, 0, 0)),
        ],
        out_specs=[
            pl.BlockSpec((1, BLOCK, width), lambda b, c, t: (b, 0, 0)),
            pl.BlockSpec((1, BLOCK, width), lambda b, c, t: (b, 0, 0)),
        ],
    )
    flops = blocks * (width // 128) * 2 * 4 * 2 * BLOCK * 128 * keys
    cost = pl.CostEstimate(flops=flops, transcendentals=blocks * HEADS * BLOCK * keys,
                           bytes_accessed=qg_blocks.size * 2 + st.size * 4 + 6 * blocks * BLOCK * width * 4)
    return pl.pallas_call(
        functools.partial(key_side_kernel, scale=scale),
        grid_spec=grid_spec,
        out_shape=[jax.ShapeDtypeStruct((blocks, BLOCK, width), jnp.float32)] * 2,
        cost_estimate=cost,
    )(tile_count, tiles, qg_blocks, st, k3, v3)


def shards(query, key, value, out_grad, partner, tiles, tile_count):
    f32 = jnp.float32
    bf16 = jnp.bfloat16
    nodes, width = query.shape
    head_dim = width // HEADS
    scale = head_dim ** (-0.5)
    blocks_dev = nodes // BLOCK
    team = lax.axis_size("blk")
    cluster_blocks = blocks_dev * team

    both = jnp.concatenate([key, value], 1)
    kv_cluster = lax.all_gather(both, "blk", axis=0, tiled=True)
    qg_cluster = lax.all_gather(jnp.concatenate([query, out_grad], 1), "blk", axis=0, tiled=True)
    partner_rows = jnp.stack(
        [fetch_partners(both, partner[step], step + 1) for step in range(ROUNDS)]
    )

    out_full, query_grad, terms, stats = query_side(
        tile_count,
        tiles,
        kv_cluster.reshape(cluster_blocks, BLOCK, 2 * width),
        query.reshape(blocks_dev, BLOCK, width),
        out_grad.reshape(blocks_dev, BLOCK, width),
        partner_rows.reshape(ROUNDS, blocks_dev, BLOCK, 2 * width),
        scale,
    )

    stats = stats[..., : 3 * HEADS].reshape(blocks_dev, BLOCK, 3, HEADS)
    stats = jnp.transpose(stats, (0, 2, 3, 1)).reshape(blocks_dev * 3 * HEADS, BLOCK)
    stats_cluster = lax.all_gather(stats, "blk", axis=0, tiled=True)

    terms = terms.reshape(ROUNDS, nodes, 2 * width)
    returned = jnp.stack(
        [fetch_partners(terms[step], partner[step], step + 1) for step in range(ROUNDS)]
    )
    returned = jnp.sum(returned.astype(f32), 0)
    returned, stats_cluster, qg_cluster = lax.optimization_barrier(
        (returned, stats_cluster, qg_cluster)
    )

    k_sum, v_sum = key_side(
        tile_count,
        tiles,
        qg_cluster.reshape(cluster_blocks, BLOCK, 2 * width),
        stats_cluster.reshape(cluster_blocks, 3, HEADS, BLOCK),
        key.reshape(blocks_dev, BLOCK, width),
        value.reshape(blocks_dev, BLOCK, width),
        scale,
    )

    attended = out_full.reshape(nodes, width).astype(bf16)
    query_grad = query_grad.reshape(nodes, width)
    key_grad = (k_sum.reshape(nodes, width) + returned[:, :width]).astype(bf16)
    value_grad = (v_sum.reshape(nodes, width) + returned[:, width:]).astype(bf16)
    return (attended, query_grad, key_grad, value_grad)


def solution(mesh):
    in_specs = (
        P(("grp", "blk"), None),
        P(("grp", "blk"), None),
        P(("grp", "blk"), None),
        P(("grp", "blk"), None),
        P(None, ("grp", "blk")),
        P(("grp", "blk"), None),
        P(("grp", "blk")),
    )
    out_specs = (
        P(("grp", "blk"), None),
        P(("grp", "blk"), None),
        P(("grp", "blk"), None),
        P(("grp", "blk"), None),
    )
    return jax.shard_map(shards, mesh=mesh, in_specs=in_specs, out_specs=out_specs, check_vma=False)
```

```python
import functools

import jax
import jax.numpy as jnp
from jax import lax
from jax.experimental import pallas as pl
from jax.experimental.pallas import tpu as pltpu
from jax.sharding import PartitionSpec as P

HEADS = 8
BLOCK = 128
TMAX = 6
ROUNDS = 2


NEG_BIG = -1e30


def passed_along(x, axis, by):
    size = lax.axis_size(axis)
    return lax.ppermute(x, axis, [(i, (i + by) % size) for i in range(size)])


def fetch_partners(load, slots, offset):
    half = load.shape[0] // 2
    ahead = passed_along(load[half:], "grp", -offset)
    behind = passed_along(load[:half], "grp", offset)
    return jnp.concatenate([ahead[slots[:half]], behind[slots[half:]]], 0)


def query_side_kernel(
    count_ref, tiles_ref, kv_ref, q_ref, g_ref, pair_ref, out_ref, qgrad_ref, term_ref, st_ref, *, scale
):
    b = pl.program_id(0)
    width = q_ref.shape[-1]
    slots = tiles_ref.shape[1]
    keys = slots * BLOCK
    ids = [tiles_ref[b, t] for t in range(slots)]
    pair = 2 * (width // HEADS)
    half = pair // 2
    f32, bf16 = jnp.float32, jnp.bfloat16
    live = (lax.broadcasted_iota(jnp.int32, (1, keys), 1) // BLOCK) < count_ref[b]
    low = lax.broadcasted_iota(jnp.int32, (1, pair), 1) < half
    lane = lax.broadcasted_iota(jnp.int32, (1, pair), 1)
    nt = (((1,), (1,)), ((), ()))
    stats = jnp.zeros((BLOCK, pair), f32)
    for pr in range(width // pair):
        cols = pl.ds(pr * pair, pair)
        qp = q_ref[0, :, cols]
        gp = g_ref[0, :, cols]
        kp = jnp.concatenate([kv_ref[i, :, cols] for i in ids], 0)
        vp = jnp.concatenate([kv_ref[i, :, pl.ds(width + pr * pair, pair)] for i in ids], 0)
        kr = [pair_ref[r, 0, :, cols].astype(f32) for r in range(ROUNDS)]
        vr = [pair_ref[r, 0, :, pl.ds(width + pr * pair, pair)].astype(f32) for r in range(ROUNDS)]
        qf = qp.astype(f32)
        gf = gp.astype(f32)
        outs, grads = [], []
        tk = [[] for _ in range(ROUNDS)]
        tv = [[] for _ in range(ROUNDS)]
        for side in range(2):
            mine = low if side == 0 else jnp.logical_not(low)
            h = 2 * pr + side
            qh = jnp.where(mine, qp, jnp.zeros_like(qp))
            gh = jnp.where(mine, gp, jnp.zeros_like(gp))
            qhf = jnp.where(mine, qf, 0.0)
            ghf = jnp.where(mine, gf, 0.0)
            s_loc = lax.dot_general(qh, kp, nt, preferred_element_type=f32) * scale
            s_loc = jnp.where(live, s_loc, NEG_BIG)
            s_pair = [jnp.sum(qhf * kr[r], -1, keepdims=True) * scale for r in range(ROUNDS)]
            top = jnp.max(s_loc, -1, keepdims=True)
            for r in range(ROUNDS):
                top = jnp.maximum(top, s_pair[r])
            e_loc = jnp.exp(s_loc - top)
            e_pair = [jnp.exp(s_pair[r] - top) for r in range(ROUNDS)]
            total = jnp.sum(e_loc, -1, keepdims=True)
            for r in range(ROUNDS):
                total = total + e_pair[r]
            p_loc = e_loc / total
            p_pair = [e_pair[r] / total for r in range(ROUNDS)]
            w_loc = p_loc.astype(bf16)
            w_pair = [p_pair[r].astype(bf16).astype(f32) for r in range(ROUNDS)]
            out = jnp.dot(w_loc, vp, preferred_element_type=f32)
            for r in range(ROUNDS):
                out = out + w_pair[r] * vr[r]
            delta = jnp.sum(jnp.where(mine, gf * out, 0.0), -1, keepdims=True)
            d_loc = lax.dot_general(gh, vp, nt, preferred_element_type=f32)
            d_pair = [jnp.sum(ghf * vr[r], -1, keepdims=True) for r in range(ROUNDS)]
            z_loc = (p_loc * (d_loc - delta)).astype(bf16)
            z_pair = [(p_pair[r] * (d_pair[r] - delta)).astype(bf16).astype(f32) for r in range(ROUNDS)]
            grad = jnp.dot(z_loc, kp, preferred_element_type=f32)
            for r in range(ROUNDS):
                grad = grad + z_pair[r] * kr[r]
            outs.append(out)
            grads.append(grad * scale)
            for r in range(ROUNDS):
                tk[r].append(z_pair[r] * qf * scale)
                tv[r].append(w_pair[r] * gf)
            for i, value in enumerate((top, total, delta)):
                stats = jnp.where(lane == i * HEADS + h, value, stats)
        out_ref[0, :, cols] = jnp.where(low, outs[0], outs[1])
        qgrad_ref[0, :, cols] = jnp.where(low, grads[0], grads[1]).astype(bf16)
        for r in range(ROUNDS):
            term_ref[r, 0, :, cols] = jnp.where(low, tk[r][0], tk[r][1]).astype(bf16)
            term_ref[r, 0, :, pl.ds(width + pr * pair, pair)] = jnp.where(low, tv[r][0], tv[r][1]).astype(bf16)
    st_ref[0] = stats


def query_side(tile_count, tiles, kv_blocks, q3, g3, pair_rows, scale):
    blocks, slots = tiles.shape
    keys = slots * BLOCK
    width2 = kv_blocks.shape[-1]
    width = width2 // 2
    grid_spec = pltpu.PrefetchScalarGridSpec(
        num_scalar_prefetch=2,
        grid=(blocks,),
        in_specs=[
            pl.BlockSpec(memory_space=pltpu.VMEM),
            pl.BlockSpec((1, BLOCK, width), lambda b, c, t: (b, 0, 0)),
            pl.BlockSpec((1, BLOCK, width), lambda b, c, t: (b, 0, 0)),
            pl.BlockSpec((ROUNDS, 1, BLOCK, width2), lambda b, c, t: (0, b, 0, 0)),
        ],
        out_specs=[
            pl.BlockSpec((1, BLOCK, width), lambda b, c, t: (b, 0, 0)),
            pl.BlockSpec((1, BLOCK, width), lambda b, c, t: (b, 0, 0)),
            pl.BlockSpec((ROUNDS, 1, BLOCK, width2), lambda b, c, t: (0, b, 0, 0)),
            pl.BlockSpec((1, BLOCK, 2 * (width // HEADS)), lambda b, c, t: (b, 0, 0)),
        ],
    )
    flops = blocks * (width // 128) * 2 * 4 * 2 * BLOCK * 128 * keys
    cost = pl.CostEstimate(flops=flops, transcendentals=blocks * HEADS * BLOCK * keys,
                           bytes_accessed=kv_blocks.size * 2 + pair_rows.size * 2 + 8 * blocks * BLOCK * width * 4)
    return pl.pallas_call(
        functools.partial(query_side_kernel, scale=scale),
        grid_spec=grid_spec,
        out_shape=[
            jax.ShapeDtypeStruct((blocks, BLOCK, width), jnp.float32),
            jax.ShapeDtypeStruct((blocks, BLOCK, width), jnp.bfloat16),
            jax.ShapeDtypeStruct((ROUNDS, blocks, BLOCK, width2), jnp.bfloat16),
            jax.ShapeDtypeStruct((blocks, BLOCK, 2 * (width // HEADS)), jnp.float32),
        ],
        cost_estimate=cost,
    )(tile_count, tiles, kv_blocks, q3, g3, pair_rows)


def key_side_kernel(count_ref, tiles_ref, qg_ref, st_ref, k_ref, v_ref, ks_ref, vs_ref, *, scale):
    b = pl.program_id(0)
    width = k_ref.shape[-1]
    slots = tiles_ref.shape[1]
    keys = slots * BLOCK
    ids = [tiles_ref[b, t] for t in range(slots)]
    pair = 2 * (width // HEADS)
    half = pair // 2
    live = (lax.broadcasted_iota(jnp.int32, (1, keys), 1) // BLOCK) < count_ref[b]
    low = lax.broadcasted_iota(jnp.int32, (1, pair), 1) < half
    nt = (((1,), (1,)), ((), ()))
    for pr in range(width // pair):
        cols = pl.ds(pr * pair, pair)
        kp = k_ref[0, :, cols]
        vp = v_ref[0, :, cols]
        qp = jnp.concatenate([qg_ref[i, :, cols] for i in ids], 0)
        gp = jnp.concatenate([qg_ref[i, :, pl.ds(width + pr * pair, pair)] for i in ids], 0)
        zero = jnp.zeros_like(kp)
        k_out = []
        v_out = []
        for side in range(2):
            mine = low if side == 0 else jnp.logical_not(low)
            h = 2 * pr + side
            kh = jnp.where(mine, kp, zero)
            vh = jnp.where(mine, vp, zero)
            s = lax.dot_general(kh, qp, nt, preferred_element_type=jnp.float32) * scale
            d = lax.dot_general(vh, gp, nt, preferred_element_type=jnp.float32)
            top, total, delta = [
                jnp.concatenate([st_ref[i, j, pl.ds(h, 1), :] for i in ids], 1) for j in range(3)
            ]
            p = jnp.where(live, jnp.exp(s - top) / total, 0.0)
            w = p.astype(jnp.bfloat16)
            z = (p * (d - delta)).astype(jnp.bfloat16)
            k_out.append(jnp.dot(z, qp, preferred_element_type=jnp.float32))
            v_out.append(jnp.dot(w, gp, preferred_element_type=jnp.float32))
        ks_ref[0, :, cols] = jnp.where(low, k_out[0], k_out[1]) * scale
        vs_ref[0, :, cols] = jnp.where(low, v_out[0], v_out[1])


def key_side(tile_count, tiles, qg_blocks, st, k3, v3, scale):
    blocks, slots = tiles.shape
    keys = slots * BLOCK
    width = k3.shape[-1]
    grid_spec = pltpu.PrefetchScalarGridSpec(
        num_scalar_prefetch=2,
        grid=(blocks,),
        in_specs=[
            pl.BlockSpec(memory_space=pltpu.VMEM),
            pl.BlockSpec(memory_space=pltpu.VMEM),
            pl.BlockSpec((1, BLOCK, width), lambda b, c, t: (b, 0, 0)),
            pl.BlockSpec((1, BLOCK, width), lambda b, c, t: (b, 0, 0)),
        ],
        out_specs=[
            pl.BlockSpec((1, BLOCK, width), lambda b, c, t: (b, 0, 0)),
            pl.BlockSpec((1, BLOCK, width), lambda b, c, t: (b, 0, 0)),
        ],
    )
    flops = blocks * (width // 128) * 2 * 4 * 2 * BLOCK * 128 * keys
    cost = pl.CostEstimate(flops=flops, transcendentals=blocks * HEADS * BLOCK * keys,
                           bytes_accessed=qg_blocks.size * 2 + st.size * 4 + 6 * blocks * BLOCK * width * 4)
    return pl.pallas_call(
        functools.partial(key_side_kernel, scale=scale),
        grid_spec=grid_spec,
        out_shape=[jax.ShapeDtypeStruct((blocks, BLOCK, width), jnp.float32)] * 2,
        cost_estimate=cost,
    )(tile_count, tiles, qg_blocks, st, k3, v3)


def doubling_gather(x, axis):
    size = lax.axis_size(axis)
    me = lax.axis_index(axis)
    step = 1
    while step < size:
        other = lax.ppermute(x, axis, [(i, i ^ step) for i in range(size)])
        x = jnp.where((me & step) == 0, jnp.concatenate([x, other], 0), jnp.concatenate([other, x], 0))
        step *= 2
    return x


def shards(query, key, value, out_grad, partner, tiles, tile_count):
    f32 = jnp.float32
    bf16 = jnp.bfloat16
    nodes, width = query.shape
    head_dim = width // HEADS
    scale = head_dim ** (-0.5)
    blocks_dev = nodes // BLOCK
    team = lax.axis_size("blk")
    cluster_blocks = blocks_dev * team

    both = jnp.concatenate([key, value], 1)
    kv_cluster = lax.all_gather(both, "blk", axis=0, tiled=True)
    qg_cluster = lax.all_gather(jnp.concatenate([query, out_grad], 1), "blk", axis=0, tiled=True)
    partner_rows = jnp.stack(
        [fetch_partners(both, partner[step], step + 1) for step in range(ROUNDS)]
    )

    out_full, query_grad, terms, stats = query_side(
        tile_count,
        tiles,
        kv_cluster.reshape(cluster_blocks, BLOCK, 2 * width),
        query.reshape(blocks_dev, BLOCK, width),
        out_grad.reshape(blocks_dev, BLOCK, width),
        partner_rows.reshape(ROUNDS, blocks_dev, BLOCK, 2 * width),
        scale,
    )

    stats = stats[..., : 3 * HEADS].reshape(blocks_dev, BLOCK, 3, HEADS)
    stats = jnp.transpose(stats, (0, 2, 3, 1)).reshape(blocks_dev * 3 * HEADS, BLOCK)
    stats_cluster = doubling_gather(stats, "blk")

    terms = terms.reshape(ROUNDS, nodes, 2 * width)
    returned = jnp.stack(
        [fetch_partners(terms[step], partner[step], step + 1) for step in range(ROUNDS)]
    )
    returned = jnp.sum(returned.astype(f32), 0)
    returned, stats_cluster, qg_cluster = lax.optimization_barrier(
        (returned, stats_cluster, qg_cluster)
    )

    k_sum, v_sum = key_side(
        tile_count,
        tiles,
        qg_cluster.reshape(cluster_blocks, BLOCK, 2 * width),
        stats_cluster.reshape(cluster_blocks, 3, HEADS, BLOCK),
        key.reshape(blocks_dev, BLOCK, width),
        value.reshape(blocks_dev, BLOCK, width),
        scale,
    )

    attended = out_full.reshape(nodes, width).astype(bf16)
    query_grad = query_grad.reshape(nodes, width)
    key_grad = (k_sum.reshape(nodes, width) + returned[:, :width]).astype(bf16)
    value_grad = (v_sum.reshape(nodes, width) + returned[:, width:]).astype(bf16)
    return (attended, query_grad, key_grad, value_grad)


def solution(mesh):
    in_specs = (
        P(("grp", "blk"), None),
        P(("grp", "blk"), None),
        P(("grp", "blk"), None),
        P(("grp", "blk"), None),
        P(None, ("grp", "blk")),
        P(("grp", "blk"), None),
        P(("grp", "blk")),
    )
    out_specs = (
        P(("grp", "blk"), None),
        P(("grp", "blk"), None),
        P(("grp", "blk"), None),
        P(("grp", "blk"), None),
    )
    return jax.shard_map(shards, mesh=mesh, in_specs=in_specs, out_specs=out_specs, check_vma=False)
```

```python
import functools

import jax
import jax.numpy as jnp
from jax import lax
from jax.experimental import pallas as pl
from jax.experimental.pallas import tpu as pltpu
from jax.sharding import PartitionSpec as P

HEADS = 8
BLOCK = 128
TMAX = 6
ROUNDS = 2


NEG_BIG = -1e30


def passed_along(x, axis, by):
    size = lax.axis_size(axis)
    return lax.ppermute(x, axis, [(i, (i + by) % size) for i in range(size)])


def fetch_partners(load, slots, offset):
    half = load.shape[0] // 2
    ahead = passed_along(load[half:], "grp", -offset)
    behind = passed_along(load[:half], "grp", offset)
    return jnp.concatenate([ahead[slots[:half]], behind[slots[half:]]], 0)


def query_side_kernel(
    count_ref, tiles_ref, kv_ref, q_ref, g_ref, pair_ref, out_ref, qgrad_ref, term_ref, st_ref, *, scale
):
    b = pl.program_id(0)
    width = q_ref.shape[-1]
    slots = tiles_ref.shape[1]
    keys = slots * BLOCK
    ids = [tiles_ref[b, t] for t in range(slots)]
    pair = 2 * (width // HEADS)
    half = pair // 2
    f32, bf16 = jnp.float32, jnp.bfloat16
    live = (lax.broadcasted_iota(jnp.int32, (1, keys), 1) // BLOCK) < count_ref[b]
    low = lax.broadcasted_iota(jnp.int32, (1, pair), 1) < half
    lane = lax.broadcasted_iota(jnp.int32, (1, pair), 1)
    nt = (((1,), (1,)), ((), ()))
    stats = jnp.zeros((BLOCK, pair), f32)
    for pr in range(width // pair):
        cols = pl.ds(pr * pair, pair)
        qp = q_ref[0, :, cols]
        gp = g_ref[0, :, cols]
        kp = jnp.concatenate([kv_ref[i, :, cols] for i in ids], 0)
        vp = jnp.concatenate([kv_ref[i, :, pl.ds(width + pr * pair, pair)] for i in ids], 0)
        kr = [pair_ref[r, 0, :, cols].astype(f32) for r in range(ROUNDS)]
        vr = [pair_ref[r, 0, :, pl.ds(width + pr * pair, pair)].astype(f32) for r in range(ROUNDS)]
        qf = qp.astype(f32)
        gf = gp.astype(f32)
        outs, grads = [], []
        tk = [[] for _ in range(ROUNDS)]
        tv = [[] for _ in range(ROUNDS)]
        for side in range(2):
            mine = low if side == 0 else jnp.logical_not(low)
            h = 2 * pr + side
            qh = jnp.where(mine, qp, jnp.zeros_like(qp))
            gh = jnp.where(mine, gp, jnp.zeros_like(gp))
            qhf = jnp.where(mine, qf, 0.0)
            ghf = jnp.where(mine, gf, 0.0)
            s_loc = lax.dot_general(qh, kp, nt, preferred_element_type=f32) * scale
            s_loc = jnp.where(live, s_loc, NEG_BIG)
            s_pair = [jnp.sum(qhf * kr[r], -1, keepdims=True) * scale for r in range(ROUNDS)]
            top = jnp.max(s_loc, -1, keepdims=True)
            for r in range(ROUNDS):
                top = jnp.maximum(top, s_pair[r])
            e_loc = jnp.exp(s_loc - top)
            e_pair = [jnp.exp(s_pair[r] - top) for r in range(ROUNDS)]
            total = jnp.sum(e_loc, -1, keepdims=True)
            for r in range(ROUNDS):
                total = total + e_pair[r]
            p_loc = e_loc / total
            p_pair = [e_pair[r] / total for r in range(ROUNDS)]
            w_loc = p_loc.astype(bf16)
            w_pair = [p_pair[r].astype(bf16).astype(f32) for r in range(ROUNDS)]
            out = jnp.dot(w_loc, vp, preferred_element_type=f32)
            for r in range(ROUNDS):
                out = out + w_pair[r] * vr[r]
            delta = jnp.sum(jnp.where(mine, gf * out, 0.0), -1, keepdims=True)
            d_loc = lax.dot_general(gh, vp, nt, preferred_element_type=f32)
            d_pair = [jnp.sum(ghf * vr[r], -1, keepdims=True) for r in range(ROUNDS)]
            z_loc = (p_loc * (d_loc - delta)).astype(bf16)
            z_pair = [(p_pair[r] * (d_pair[r] - delta)).astype(bf16).astype(f32) for r in range(ROUNDS)]
            grad = jnp.dot(z_loc, kp, preferred_element_type=f32)
            for r in range(ROUNDS):
                grad = grad + z_pair[r] * kr[r]
            outs.append(out)
            grads.append(grad * scale)
            for r in range(ROUNDS):
                tk[r].append(z_pair[r] * qf * scale)
                tv[r].append(w_pair[r] * gf)
            for i, value in enumerate((top, total, delta)):
                stats = jnp.where(lane == i * HEADS + h, value, stats)
        out_ref[0, :, cols] = jnp.where(low, outs[0], outs[1])
        qgrad_ref[0, :, cols] = jnp.where(low, grads[0], grads[1]).astype(bf16)
        for r in range(ROUNDS):
            term_ref[r, 0, :, cols] = jnp.where(low, tk[r][0], tk[r][1]).astype(bf16)
            term_ref[r, 0, :, pl.ds(width + pr * pair, pair)] = jnp.where(low, tv[r][0], tv[r][1]).astype(bf16)
    st_ref[0] = stats


def query_side(tile_count, tiles, kv_blocks, q3, g3, pair_rows, scale):
    blocks, slots = tiles.shape
    keys = slots * BLOCK
    width2 = kv_blocks.shape[-1]
    width = width2 // 2
    grid_spec = pltpu.PrefetchScalarGridSpec(
        num_scalar_prefetch=2,
        grid=(blocks,),
        in_specs=[
            pl.BlockSpec(memory_space=pltpu.VMEM),
            pl.BlockSpec((1, BLOCK, width), lambda b, c, t: (b, 0, 0)),
            pl.BlockSpec((1, BLOCK, width), lambda b, c, t: (b, 0, 0)),
            pl.BlockSpec((ROUNDS, 1, BLOCK, width2), lambda b, c, t: (0, b, 0, 0)),
        ],
        out_specs=[
            pl.BlockSpec((1, BLOCK, width), lambda b, c, t: (b, 0, 0)),
            pl.BlockSpec((1, BLOCK, width), lambda b, c, t: (b, 0, 0)),
            pl.BlockSpec((ROUNDS, 1, BLOCK, width2), lambda b, c, t: (0, b, 0, 0)),
            pl.BlockSpec((1, BLOCK, 2 * (width // HEADS)), lambda b, c, t: (b, 0, 0)),
        ],
    )
    flops = blocks * (width // 128) * 2 * 4 * 2 * BLOCK * 128 * keys
    cost = pl.CostEstimate(flops=flops, transcendentals=blocks * HEADS * BLOCK * keys,
                           bytes_accessed=kv_blocks.size * 2 + pair_rows.size * 2 + 8 * blocks * BLOCK * width * 4)
    return pl.pallas_call(
        functools.partial(query_side_kernel, scale=scale),
        grid_spec=grid_spec,
        out_shape=[
            jax.ShapeDtypeStruct((blocks, BLOCK, width), jnp.float32),
            jax.ShapeDtypeStruct((blocks, BLOCK, width), jnp.bfloat16),
            jax.ShapeDtypeStruct((ROUNDS, blocks, BLOCK, width2), jnp.bfloat16),
            jax.ShapeDtypeStruct((blocks, BLOCK, 2 * (width // HEADS)), jnp.float32),
        ],
        cost_estimate=cost,
    )(tile_count, tiles, kv_blocks, q3, g3, pair_rows)


def key_side_kernel(count_ref, tiles_ref, qg_ref, st_ref, k_ref, v_ref, ret_ref, ks_ref, vs_ref, *, scale):
    b = pl.program_id(0)
    width = k_ref.shape[-1]
    slots = tiles_ref.shape[1]
    keys = slots * BLOCK
    ids = [tiles_ref[b, t] for t in range(slots)]
    pair = 2 * (width // HEADS)
    half = pair // 2
    live = (lax.broadcasted_iota(jnp.int32, (1, keys), 1) // BLOCK) < count_ref[b]
    low = lax.broadcasted_iota(jnp.int32, (1, pair), 1) < half
    nt = (((1,), (1,)), ((), ()))
    for pr in range(width // pair):
        cols = pl.ds(pr * pair, pair)
        kp = k_ref[0, :, cols]
        vp = v_ref[0, :, cols]
        qp = jnp.concatenate([qg_ref[i, :, cols] for i in ids], 0)
        gp = jnp.concatenate([qg_ref[i, :, pl.ds(width + pr * pair, pair)] for i in ids], 0)
        zero = jnp.zeros_like(kp)
        k_out = []
        v_out = []
        for side in range(2):
            mine = low if side == 0 else jnp.logical_not(low)
            h = 2 * pr + side
            kh = jnp.where(mine, kp, zero)
            vh = jnp.where(mine, vp, zero)
            s = lax.dot_general(kh, qp, nt, preferred_element_type=jnp.float32) * scale
            d = lax.dot_general(vh, gp, nt, preferred_element_type=jnp.float32)
            top, total, delta = [
                jnp.concatenate([st_ref[i, j, pl.ds(h, 1), :] for i in ids], 1) for j in range(3)
            ]
            p = jnp.where(live, jnp.exp(s - top) / total, 0.0)
            w = p.astype(jnp.bfloat16)
            z = (p * (d - delta)).astype(jnp.bfloat16)
            k_out.append(jnp.dot(z, qp, preferred_element_type=jnp.float32))
            v_out.append(jnp.dot(w, gp, preferred_element_type=jnp.float32))
        k_sum = jnp.where(low, k_out[0], k_out[1]) * scale
        v_sum = jnp.where(low, v_out[0], v_out[1])
        ks_ref[0, :, cols] = (k_sum + ret_ref[0, :, cols]).astype(ks_ref.dtype)
        vs_ref[0, :, cols] = (v_sum + ret_ref[0, :, pl.ds(width + pr * pair, pair)]).astype(vs_ref.dtype)


def key_side(tile_count, tiles, qg_blocks, st, k3, v3, returned, scale):
    blocks, slots = tiles.shape
    keys = slots * BLOCK
    width = k3.shape[-1]
    grid_spec = pltpu.PrefetchScalarGridSpec(
        num_scalar_prefetch=2,
        grid=(blocks,),
        in_specs=[
            pl.BlockSpec(memory_space=pltpu.VMEM),
            pl.BlockSpec(memory_space=pltpu.VMEM),
            pl.BlockSpec((1, BLOCK, width), lambda b, c, t: (b, 0, 0)),
            pl.BlockSpec((1, BLOCK, width), lambda b, c, t: (b, 0, 0)),
            pl.BlockSpec((1, BLOCK, 2 * width), lambda b, c, t: (b, 0, 0)),
        ],
        out_specs=[
            pl.BlockSpec((1, BLOCK, width), lambda b, c, t: (b, 0, 0)),
            pl.BlockSpec((1, BLOCK, width), lambda b, c, t: (b, 0, 0)),
        ],
    )
    flops = blocks * (width // 128) * 2 * 4 * 2 * BLOCK * 128 * keys
    cost = pl.CostEstimate(flops=flops, transcendentals=blocks * HEADS * BLOCK * keys,
                           bytes_accessed=qg_blocks.size * 2 + st.size * 4 + 6 * blocks * BLOCK * width * 4)
    return pl.pallas_call(
        functools.partial(key_side_kernel, scale=scale),
        grid_spec=grid_spec,
        out_shape=[jax.ShapeDtypeStruct((blocks, BLOCK, width), jnp.bfloat16)] * 2,
        cost_estimate=cost,
    )(tile_count, tiles, qg_blocks, st, k3, v3, returned)


def doubling_gather(x, axis):
    size = lax.axis_size(axis)
    me = lax.axis_index(axis)
    step = 1
    while step < size:
        other = lax.ppermute(x, axis, [(i, i ^ step) for i in range(size)])
        x = jnp.where((me & step) == 0, jnp.concatenate([x, other], 0), jnp.concatenate([other, x], 0))
        step *= 2
    return x


def shards(query, key, value, out_grad, partner, tiles, tile_count):
    f32 = jnp.float32
    bf16 = jnp.bfloat16
    nodes, width = query.shape
    head_dim = width // HEADS
    scale = head_dim ** (-0.5)
    blocks_dev = nodes // BLOCK
    team = lax.axis_size("blk")
    cluster_blocks = blocks_dev * team

    both = jnp.concatenate([key, value], 1)
    kv_cluster = lax.all_gather(both, "blk", axis=0, tiled=True)
    qg_cluster = lax.all_gather(jnp.concatenate([query, out_grad], 1), "blk", axis=0, tiled=True)
    partner_rows = jnp.stack(
        [fetch_partners(both, partner[step], step + 1) for step in range(ROUNDS)]
    )

    out_full, query_grad, terms, stats = query_side(
        tile_count,
        tiles,
        kv_cluster.reshape(cluster_blocks, BLOCK, 2 * width),
        query.reshape(blocks_dev, BLOCK, width),
        out_grad.reshape(blocks_dev, BLOCK, width),
        partner_rows.reshape(ROUNDS, blocks_dev, BLOCK, 2 * width),
        scale,
    )

    stats = stats[..., : 3 * HEADS].reshape(blocks_dev, BLOCK, 3, HEADS)
    stats = jnp.transpose(stats, (0, 2, 3, 1)).reshape(blocks_dev * 3 * HEADS, BLOCK)
    stats_cluster = doubling_gather(stats, "blk")

    terms = terms.reshape(ROUNDS, nodes, 2 * width)
    returned = jnp.stack(
        [fetch_partners(terms[step], partner[step], step + 1) for step in range(ROUNDS)]
    )
    returned = jnp.sum(returned.astype(f32), 0)
    returned, stats_cluster, qg_cluster = lax.optimization_barrier(
        (returned, stats_cluster, qg_cluster)
    )

    key_grad, value_grad = key_side(
        tile_count,
        tiles,
        qg_cluster.reshape(cluster_blocks, BLOCK, 2 * width),
        stats_cluster.reshape(cluster_blocks, 3, HEADS, BLOCK),
        key.reshape(blocks_dev, BLOCK, width),
        value.reshape(blocks_dev, BLOCK, width),
        returned.reshape(blocks_dev, BLOCK, 2 * width),
        scale,
    )

    attended = out_full.reshape(nodes, width).astype(bf16)
    query_grad = query_grad.reshape(nodes, width)
    key_grad = key_grad.reshape(nodes, width)
    value_grad = value_grad.reshape(nodes, width)
    return (attended, query_grad, key_grad, value_grad)


def solution(mesh):
    in_specs = (
        P(("grp", "blk"), None),
        P(("grp", "blk"), None),
        P(("grp", "blk"), None),
        P(("grp", "blk"), None),
        P(None, ("grp", "blk")),
        P(("grp", "blk"), None),
        P(("grp", "blk")),
    )
    out_specs = (
        P(("grp", "blk"), None),
        P(("grp", "blk"), None),
        P(("grp", "blk"), None),
        P(("grp", "blk"), None),
    )
    return jax.shard_map(shards, mesh=mesh, in_specs=in_specs, out_specs=out_specs, check_vma=False)
```

```python
import functools

import jax
import jax.numpy as jnp
from jax import lax
from jax.experimental import pallas as pl
from jax.experimental.pallas import tpu as pltpu
from jax.sharding import PartitionSpec as P

HEADS = 8
BLOCK = 128
TMAX = 6
ROUNDS = 2


NEG_BIG = -1e30


def passed_along(x, axis, by):
    size = lax.axis_size(axis)
    return lax.ppermute(x, axis, [(i, (i + by) % size) for i in range(size)])


def fetch_partners(load, slots, offset):
    half = load.shape[0] // 2
    ahead = passed_along(load[half:], "grp", -offset)
    behind = passed_along(load[:half], "grp", offset)
    return jnp.concatenate([ahead[slots[:half]], behind[slots[half:]]], 0)


def query_side_kernel(
    count_ref, tiles_ref, kv_ref, q_ref, g_ref, pair_ref, out_ref, qgrad_ref, term_ref, st_ref, *, scale
):
    b = pl.program_id(0)
    width = q_ref.shape[-1]
    slots = tiles_ref.shape[1]
    keys = slots * BLOCK
    ids = [tiles_ref[b, t] for t in range(slots)]
    pair = 2 * (width // HEADS)
    half = pair // 2
    f32, bf16 = jnp.float32, jnp.bfloat16
    live = (lax.broadcasted_iota(jnp.int32, (1, keys), 1) // BLOCK) < count_ref[b]
    low = lax.broadcasted_iota(jnp.int32, (1, pair), 1) < half
    lane = lax.broadcasted_iota(jnp.int32, (1, pair), 1)
    nt = (((1,), (1,)), ((), ()))
    stats = jnp.zeros((BLOCK, pair), f32)
    for pr in range(width // pair):
        cols = pl.ds(pr * pair, pair)
        qp = q_ref[0, :, cols]
        gp = g_ref[0, :, cols]
        kp = jnp.concatenate([kv_ref[i, :, cols] for i in ids], 0)
        vp = jnp.concatenate([kv_ref[i, :, pl.ds(width + pr * pair, pair)] for i in ids], 0)
        kr = [pair_ref[r, 0, :, cols].astype(f32) for r in range(ROUNDS)]
        vr = [pair_ref[r, 0, :, pl.ds(width + pr * pair, pair)].astype(f32) for r in range(ROUNDS)]
        qf = qp.astype(f32)
        gf = gp.astype(f32)
        outs, grads = [], []
        tk = [[] for _ in range(ROUNDS)]
        tv = [[] for _ in range(ROUNDS)]
        for side in range(2):
            mine = low if side == 0 else jnp.logical_not(low)
            h = 2 * pr + side
            qh = jnp.where(mine, qp, jnp.zeros_like(qp))
            gh = jnp.where(mine, gp, jnp.zeros_like(gp))
            qhf = jnp.where(mine, qf, 0.0)
            ghf = jnp.where(mine, gf, 0.0)
            s_loc = lax.dot_general(qh, kp, nt, preferred_element_type=f32) * scale
            s_loc = jnp.where(live, s_loc, NEG_BIG)
            s_pair = [jnp.sum(qhf * kr[r], -1, keepdims=True) * scale for r in range(ROUNDS)]
            top = jnp.max(s_loc, -1, keepdims=True)
            for r in range(ROUNDS):
                top = jnp.maximum(top, s_pair[r])
            e_loc = jnp.exp(s_loc - top)
            e_pair = [jnp.exp(s_pair[r] - top) for r in range(ROUNDS)]
            total = jnp.sum(e_loc, -1, keepdims=True)
            for r in range(ROUNDS):
                total = total + e_pair[r]
            p_loc = e_loc / total
            p_pair = [e_pair[r] / total for r in range(ROUNDS)]
            w_loc = p_loc.astype(bf16)
            w_pair = [p_pair[r].astype(bf16).astype(f32) for r in range(ROUNDS)]
            out = jnp.dot(w_loc, vp, preferred_element_type=f32)
            for r in range(ROUNDS):
                out = out + w_pair[r] * vr[r]
            delta = jnp.sum(jnp.where(mine, gf * out, 0.0), -1, keepdims=True)
            d_loc = lax.dot_general(gh, vp, nt, preferred_element_type=f32)
            d_pair = [jnp.sum(ghf * vr[r], -1, keepdims=True) for r in range(ROUNDS)]
            z_loc = (p_loc * (d_loc - delta)).astype(bf16)
            z_pair = [(p_pair[r] * (d_pair[r] - delta)).astype(bf16).astype(f32) for r in range(ROUNDS)]
            grad = jnp.dot(z_loc, kp, preferred_element_type=f32)
            for r in range(ROUNDS):
                grad = grad + z_pair[r] * kr[r]
            outs.append(out)
            grads.append(grad * scale)
            for r in range(ROUNDS):
                tk[r].append(z_pair[r] * qf * scale)
                tv[r].append(w_pair[r] * gf)
            for i, value in enumerate((top, total, delta)):
                stats = jnp.where(lane == i * HEADS + h, value, stats)
        out_ref[0, :, cols] = jnp.where(low, outs[0], outs[1])
        qgrad_ref[0, :, cols] = jnp.where(low, grads[0], grads[1]).astype(bf16)
        for r in range(ROUNDS):
            term_ref[r, 0, :, cols] = jnp.where(low, tk[r][0], tk[r][1]).astype(bf16)
            term_ref[r, 0, :, pl.ds(width + pr * pair, pair)] = jnp.where(low, tv[r][0], tv[r][1]).astype(bf16)
    st_ref[0] = stats


def query_side(tile_count, tiles, kv_blocks, q3, g3, pair_rows, scale):
    blocks, slots = tiles.shape
    keys = slots * BLOCK
    width2 = kv_blocks.shape[-1]
    width = width2 // 2
    grid_spec = pltpu.PrefetchScalarGridSpec(
        num_scalar_prefetch=2,
        grid=(blocks,),
        in_specs=[
            pl.BlockSpec(memory_space=pltpu.VMEM),
            pl.BlockSpec((1, BLOCK, width), lambda b, c, t: (b, 0, 0)),
            pl.BlockSpec((1, BLOCK, width), lambda b, c, t: (b, 0, 0)),
            pl.BlockSpec((ROUNDS, 1, BLOCK, width2), lambda b, c, t: (0, b, 0, 0)),
        ],
        out_specs=[
            pl.BlockSpec((1, BLOCK, width), lambda b, c, t: (b, 0, 0)),
            pl.BlockSpec((1, BLOCK, width), lambda b, c, t: (b, 0, 0)),
            pl.BlockSpec((ROUNDS, 1, BLOCK, width2), lambda b, c, t: (0, b, 0, 0)),
            pl.BlockSpec((1, BLOCK, 2 * (width // HEADS)), lambda b, c, t: (b, 0, 0)),
        ],
    )
    flops = blocks * (width // 128) * 2 * 4 * 2 * BLOCK * 128 * keys
    cost = pl.CostEstimate(flops=flops, transcendentals=blocks * HEADS * BLOCK * keys,
                           bytes_accessed=kv_blocks.size * 2 + pair_rows.size * 2 + 8 * blocks * BLOCK * width * 4)
    return pl.pallas_call(
        functools.partial(query_side_kernel, scale=scale),
        grid_spec=grid_spec,
        out_shape=[
            jax.ShapeDtypeStruct((blocks, BLOCK, width), jnp.float32),
            jax.ShapeDtypeStruct((blocks, BLOCK, width), jnp.bfloat16),
            jax.ShapeDtypeStruct((ROUNDS, blocks, BLOCK, width2), jnp.bfloat16),
            jax.ShapeDtypeStruct((blocks, BLOCK, 2 * (width // HEADS)), jnp.float32),
        ],
        cost_estimate=cost,
    )(tile_count, tiles, kv_blocks, q3, g3, pair_rows)


def key_side_kernel(count_ref, tiles_ref, qg_ref, st_ref, k_ref, v_ref, ret_ref, ks_ref, vs_ref, *, scale):
    b = pl.program_id(0)
    width = k_ref.shape[-1]
    slots = tiles_ref.shape[1]
    keys = slots * BLOCK
    ids = [tiles_ref[b, t] for t in range(slots)]
    pair = 2 * (width // HEADS)
    half = pair // 2
    live = (lax.broadcasted_iota(jnp.int32, (1, keys), 1) // BLOCK) < count_ref[b]
    low = lax.broadcasted_iota(jnp.int32, (1, pair), 1) < half
    nt = (((1,), (1,)), ((), ()))
    for pr in range(width // pair):
        cols = pl.ds(pr * pair, pair)
        kp = k_ref[0, :, cols]
        vp = v_ref[0, :, cols]
        qp = jnp.concatenate([qg_ref[i, :, cols] for i in ids], 0)
        gp = jnp.concatenate([qg_ref[i, :, pl.ds(width + pr * pair, pair)] for i in ids], 0)
        zero = jnp.zeros_like(kp)
        k_out = []
        v_out = []
        for side in range(2):
            mine = low if side == 0 else jnp.logical_not(low)
            h = 2 * pr + side
            kh = jnp.where(mine, kp, zero)
            vh = jnp.where(mine, vp, zero)
            s = lax.dot_general(kh, qp, nt, preferred_element_type=jnp.float32) * scale
            d = lax.dot_general(vh, gp, nt, preferred_element_type=jnp.float32)
            top, total, delta = [
                jnp.concatenate([st_ref[i, j, pl.ds(h, 1), :] for i in ids], 1) for j in range(3)
            ]
            p = jnp.where(live, jnp.exp(s - top) / total, 0.0)
            w = p.astype(jnp.bfloat16)
            z = (p * (d - delta)).astype(jnp.bfloat16)
            k_out.append(jnp.dot(z, qp, preferred_element_type=jnp.float32))
            v_out.append(jnp.dot(w, gp, preferred_element_type=jnp.float32))
        k_sum = jnp.where(low, k_out[0], k_out[1]) * scale
        v_sum = jnp.where(low, v_out[0], v_out[1])
        ks_ref[0, :, cols] = (k_sum + ret_ref[0, :, cols]).astype(ks_ref.dtype)
        vs_ref[0, :, cols] = (v_sum + ret_ref[0, :, pl.ds(width + pr * pair, pair)]).astype(vs_ref.dtype)


def key_side(tile_count, tiles, qg_blocks, st, k3, v3, returned, scale):
    blocks, slots = tiles.shape
    keys = slots * BLOCK
    width = k3.shape[-1]
    grid_spec = pltpu.PrefetchScalarGridSpec(
        num_scalar_prefetch=2,
        grid=(blocks,),
        in_specs=[
            pl.BlockSpec(memory_space=pltpu.VMEM),
            pl.BlockSpec(memory_space=pltpu.VMEM),
            pl.BlockSpec((1, BLOCK, width), lambda b, c, t: (b, 0, 0)),
            pl.BlockSpec((1, BLOCK, width), lambda b, c, t: (b, 0, 0)),
            pl.BlockSpec((1, BLOCK, 2 * width), lambda b, c, t: (b, 0, 0)),
        ],
        out_specs=[
            pl.BlockSpec((1, BLOCK, width), lambda b, c, t: (b, 0, 0)),
            pl.BlockSpec((1, BLOCK, width), lambda b, c, t: (b, 0, 0)),
        ],
    )
    flops = blocks * (width // 128) * 2 * 4 * 2 * BLOCK * 128 * keys
    cost = pl.CostEstimate(flops=flops, transcendentals=blocks * HEADS * BLOCK * keys,
                           bytes_accessed=qg_blocks.size * 2 + st.size * 4 + 6 * blocks * BLOCK * width * 4)
    return pl.pallas_call(
        functools.partial(key_side_kernel, scale=scale),
        grid_spec=grid_spec,
        out_shape=[jax.ShapeDtypeStruct((blocks, BLOCK, width), jnp.bfloat16)] * 2,
        cost_estimate=cost,
    )(tile_count, tiles, qg_blocks, st, k3, v3, returned)


def doubling_gather(x, axis):
    size = lax.axis_size(axis)
    me = lax.axis_index(axis)
    bits = size.bit_length() - 1
    step = size // 2
    while step >= 1:
        other = lax.ppermute(x, axis, [(i, i ^ step) for i in range(size)])
        x = jnp.where((me & step) == 0, jnp.concatenate([x, other], 0), jnp.concatenate([other, x], 0))
        step //= 2
    pieces = x.reshape((2,) * bits + (x.shape[0] // size,) + x.shape[1:])
    order = tuple(reversed(range(bits))) + tuple(range(bits, pieces.ndim))
    return jnp.transpose(pieces, order).reshape(x.shape)


def shards(query, key, value, out_grad, partner, tiles, tile_count):
    f32 = jnp.float32
    bf16 = jnp.bfloat16
    nodes, width = query.shape
    head_dim = width // HEADS
    scale = head_dim ** (-0.5)
    blocks_dev = nodes // BLOCK
    team = lax.axis_size("blk")
    cluster_blocks = blocks_dev * team

    both = jnp.concatenate([key, value], 1)
    kv_cluster = lax.all_gather(both, "blk", axis=0, tiled=True)
    qg_cluster = lax.all_gather(jnp.concatenate([query, out_grad], 1), "blk", axis=0, tiled=True)
    partner_rows = jnp.stack(
        [fetch_partners(both, partner[step], step + 1) for step in range(ROUNDS)]
    )

    out_full, query_grad, terms, stats = query_side(
        tile_count,
        tiles,
        kv_cluster.reshape(cluster_blocks, BLOCK, 2 * width),
        query.reshape(blocks_dev, BLOCK, width),
        out_grad.reshape(blocks_dev, BLOCK, width),
        partner_rows.reshape(ROUNDS, blocks_dev, BLOCK, 2 * width),
        scale,
    )

    stats = stats[..., : 3 * HEADS].reshape(blocks_dev, BLOCK, 3, HEADS)
    stats = jnp.transpose(stats, (0, 2, 3, 1)).reshape(blocks_dev * 3 * HEADS, BLOCK)
    stats_cluster = doubling_gather(stats, "blk")

    terms = terms.reshape(ROUNDS, nodes, 2 * width)
    returned = jnp.stack(
        [fetch_partners(terms[step], partner[step], step + 1) for step in range(ROUNDS)]
    )
    returned = jnp.sum(returned.astype(f32), 0)
    returned, stats_cluster, qg_cluster = lax.optimization_barrier(
        (returned, stats_cluster, qg_cluster)
    )

    key_grad, value_grad = key_side(
        tile_count,
        tiles,
        qg_cluster.reshape(cluster_blocks, BLOCK, 2 * width),
        stats_cluster.reshape(cluster_blocks, 3, HEADS, BLOCK),
        key.reshape(blocks_dev, BLOCK, width),
        value.reshape(blocks_dev, BLOCK, width),
        returned.reshape(blocks_dev, BLOCK, 2 * width),
        scale,
    )

    attended = out_full.reshape(nodes, width).astype(bf16)
    query_grad = query_grad.reshape(nodes, width)
    key_grad = key_grad.reshape(nodes, width)
    value_grad = value_grad.reshape(nodes, width)
    return (attended, query_grad, key_grad, value_grad)


def solution(mesh):
    in_specs = (
        P(("grp", "blk"), None),
        P(("grp", "blk"), None),
        P(("grp", "blk"), None),
        P(("grp", "blk"), None),
        P(None, ("grp", "blk")),
        P(("grp", "blk"), None),
        P(("grp", "blk")),
    )
    out_specs = (
        P(("grp", "blk"), None),
        P(("grp", "blk"), None),
        P(("grp", "blk"), None),
        P(("grp", "blk"), None),
    )
    return jax.shard_map(shards, mesh=mesh, in_specs=in_specs, out_specs=out_specs, check_vma=False)
```

```python
import functools

import jax
import jax.numpy as jnp
from jax import lax
from jax.experimental import pallas as pl
from jax.experimental.pallas import tpu as pltpu
from jax.sharding import PartitionSpec as P

HEADS = 8
BLOCK = 128
TMAX = 6
ROUNDS = 2


NEG_BIG = -1e30


def passed_along(x, axis, by):
    size = lax.axis_size(axis)
    return lax.ppermute(x, axis, [(i, (i + by) % size) for i in range(size)])


def fetch_partners(load, slots, offset):
    half = load.shape[0] // 2
    ahead = passed_along(load[half:], "grp", -offset)
    behind = passed_along(load[:half], "grp", offset)
    return jnp.concatenate([ahead[slots[:half]], behind[slots[half:]]], 0)


def query_side_kernel(
    count_ref, tiles_ref, kv_ref, q_ref, g_ref, pair_ref, out_ref, qgrad_ref, term_ref, st_ref, *, scale
):
    b = pl.program_id(0)
    width = q_ref.shape[-1]
    slots = tiles_ref.shape[1]
    keys = slots * BLOCK
    ids = [tiles_ref[b, t] for t in range(slots)]
    pair = 2 * (width // HEADS)
    half = pair // 2
    f32, bf16 = jnp.float32, jnp.bfloat16
    live = (lax.broadcasted_iota(jnp.int32, (1, keys), 1) // BLOCK) < count_ref[b]
    low = lax.broadcasted_iota(jnp.int32, (1, pair), 1) < half
    lane = lax.broadcasted_iota(jnp.int32, (1, pair), 1)
    nt = (((1,), (1,)), ((), ()))
    stats = jnp.zeros((BLOCK, pair), f32)
    for pr in range(width // pair):
        cols = pl.ds(pr * pair, pair)
        qp = q_ref[0, :, cols]
        gp = g_ref[0, :, cols]
        kp = jnp.concatenate([kv_ref[i, :, cols] for i in ids], 0)
        vp = jnp.concatenate([kv_ref[i, :, pl.ds(width + pr * pair, pair)] for i in ids], 0)
        kr = [pair_ref[r, 0, :, cols].astype(f32) for r in range(ROUNDS)]
        vr = [pair_ref[r, 0, :, pl.ds(width + pr * pair, pair)].astype(f32) for r in range(ROUNDS)]
        qf = qp.astype(f32)
        gf = gp.astype(f32)
        outs, grads = [], []
        tk = [[] for _ in range(ROUNDS)]
        tv = [[] for _ in range(ROUNDS)]
        for side in range(2):
            mine = low if side == 0 else jnp.logical_not(low)
            h = 2 * pr + side
            qh = jnp.where(mine, qp, jnp.zeros_like(qp))
            gh = jnp.where(mine, gp, jnp.zeros_like(gp))
            qhf = jnp.where(mine, qf, 0.0)
            ghf = jnp.where(mine, gf, 0.0)
            s_loc = lax.dot_general(qh, kp, nt, preferred_element_type=f32) * scale
            s_loc = jnp.where(live, s_loc, NEG_BIG)
            s_pair = [jnp.sum(qhf * kr[r], -1, keepdims=True) * scale for r in range(ROUNDS)]
            top = jnp.max(s_loc, -1, keepdims=True)
            for r in range(ROUNDS):
                top = jnp.maximum(top, s_pair[r])
            e_loc = jnp.exp(s_loc - top)
            e_pair = [jnp.exp(s_pair[r] - top) for r in range(ROUNDS)]
            total = jnp.sum(e_loc, -1, keepdims=True)
            for r in range(ROUNDS):
                total = total + e_pair[r]
            p_loc = e_loc / total
            p_pair = [e_pair[r] / total for r in range(ROUNDS)]
            w_loc = p_loc.astype(bf16)
            w_pair = [p_pair[r].astype(bf16).astype(f32) for r in range(ROUNDS)]
            out = jnp.dot(w_loc, vp, preferred_element_type=f32)
            for r in range(ROUNDS):
                out = out + w_pair[r] * vr[r]
            delta = jnp.sum(jnp.where(mine, gf * out, 0.0), -1, keepdims=True)
            d_loc = lax.dot_general(gh, vp, nt, preferred_element_type=f32)
            d_pair = [jnp.sum(ghf * vr[r], -1, keepdims=True) for r in range(ROUNDS)]
            z_loc = (p_loc * (d_loc - delta)).astype(bf16)
            z_pair = [(p_pair[r] * (d_pair[r] - delta)).astype(bf16).astype(f32) for r in range(ROUNDS)]
            grad = jnp.dot(z_loc, kp, preferred_element_type=f32)
            for r in range(ROUNDS):
                grad = grad + z_pair[r] * kr[r]
            outs.append(out)
            grads.append(grad * scale)
            for r in range(ROUNDS):
                tk[r].append(z_pair[r] * qf * scale)
                tv[r].append(w_pair[r] * gf)
            for i, value in enumerate((top, total, delta)):
                stats = jnp.where(lane == i * HEADS + h, value, stats)
        out_ref[0, :, cols] = jnp.where(low, outs[0], outs[1])
        qgrad_ref[0, :, cols] = jnp.where(low, grads[0], grads[1]).astype(bf16)
        for r in range(ROUNDS):
            term_ref[r, 0, :, cols] = jnp.where(low, tk[r][0], tk[r][1]).astype(bf16)
            term_ref[r, 0, :, pl.ds(width + pr * pair, pair)] = jnp.where(low, tv[r][0], tv[r][1]).astype(bf16)
    st_ref[0] = stats


def query_side(tile_count, tiles, kv_blocks, q3, g3, pair_rows, scale):
    blocks, slots = tiles.shape
    keys = slots * BLOCK
    width2 = kv_blocks.shape[-1]
    width = width2 // 2
    grid_spec = pltpu.PrefetchScalarGridSpec(
        num_scalar_prefetch=2,
        grid=(blocks,),
        in_specs=[
            pl.BlockSpec(memory_space=pltpu.VMEM),
            pl.BlockSpec((1, BLOCK, width), lambda b, c, t: (b, 0, 0)),
            pl.BlockSpec((1, BLOCK, width), lambda b, c, t: (b, 0, 0)),
            pl.BlockSpec((ROUNDS, 1, BLOCK, width2), lambda b, c, t: (0, b, 0, 0)),
        ],
        out_specs=[
            pl.BlockSpec((1, BLOCK, width), lambda b, c, t: (b, 0, 0)),
            pl.BlockSpec((1, BLOCK, width), lambda b, c, t: (b, 0, 0)),
            pl.BlockSpec((ROUNDS, 1, BLOCK, width2), lambda b, c, t: (0, b, 0, 0)),
            pl.BlockSpec((1, BLOCK, 2 * (width // HEADS)), lambda b, c, t: (b, 0, 0)),
        ],
    )
    flops = blocks * (width // 128) * 2 * 4 * 2 * BLOCK * 128 * keys
    cost = pl.CostEstimate(flops=flops, transcendentals=blocks * HEADS * BLOCK * keys,
                           bytes_accessed=kv_blocks.size * 2 + pair_rows.size * 2 + 8 * blocks * BLOCK * width * 4)
    return pl.pallas_call(
        functools.partial(query_side_kernel, scale=scale),
        grid_spec=grid_spec,
        out_shape=[
            jax.ShapeDtypeStruct((blocks, BLOCK, width), jnp.float32),
            jax.ShapeDtypeStruct((blocks, BLOCK, width), jnp.bfloat16),
            jax.ShapeDtypeStruct((ROUNDS, blocks, BLOCK, width2), jnp.bfloat16),
            jax.ShapeDtypeStruct((blocks, BLOCK, 2 * (width // HEADS)), jnp.float32),
        ],
        cost_estimate=cost,
    )(tile_count, tiles, kv_blocks, q3, g3, pair_rows)


def key_side_kernel(count_ref, tiles_ref, qg_ref, st_ref, k_ref, v_ref, ret_ref, ks_ref, vs_ref, *, scale):
    b = pl.program_id(0)
    width = k_ref.shape[-1]
    slots = tiles_ref.shape[1]
    keys = slots * BLOCK
    ids = [tiles_ref[b, t] for t in range(slots)]
    pair = 2 * (width // HEADS)
    half = pair // 2
    live = (lax.broadcasted_iota(jnp.int32, (1, keys), 1) // BLOCK) < count_ref[b]
    low = lax.broadcasted_iota(jnp.int32, (1, pair), 1) < half
    nt = (((1,), (1,)), ((), ()))
    for pr in range(width // pair):
        cols = pl.ds(pr * pair, pair)
        kp = k_ref[0, :, cols]
        vp = v_ref[0, :, cols]
        qp = jnp.concatenate([qg_ref[i, :, cols] for i in ids], 0)
        gp = jnp.concatenate([qg_ref[i, :, pl.ds(width + pr * pair, pair)] for i in ids], 0)
        zero = jnp.zeros_like(kp)
        k_out = []
        v_out = []
        for side in range(2):
            mine = low if side == 0 else jnp.logical_not(low)
            h = 2 * pr + side
            kh = jnp.where(mine, kp, zero)
            vh = jnp.where(mine, vp, zero)
            s = lax.dot_general(kh, qp, nt, preferred_element_type=jnp.float32) * scale
            d = lax.dot_general(vh, gp, nt, preferred_element_type=jnp.float32)
            top, total, delta = [
                jnp.concatenate([st_ref[i, j, pl.ds(h, 1), :] for i in ids], 1) for j in range(3)
            ]
            p = jnp.where(live, jnp.exp(s - top) / total, 0.0)
            w = p.astype(jnp.bfloat16)
            z = (p * (d - delta)).astype(jnp.bfloat16)
            k_out.append(jnp.dot(z, qp, preferred_element_type=jnp.float32))
            v_out.append(jnp.dot(w, gp, preferred_element_type=jnp.float32))
        k_sum = jnp.where(low, k_out[0], k_out[1]) * scale
        v_sum = jnp.where(low, v_out[0], v_out[1])
        ks_ref[0, :, cols] = (k_sum + ret_ref[0, :, cols]).astype(ks_ref.dtype)
        vs_ref[0, :, cols] = (v_sum + ret_ref[0, :, pl.ds(width + pr * pair, pair)]).astype(vs_ref.dtype)


def key_side(tile_count, tiles, qg_blocks, st, k3, v3, returned, scale, out_dtype=jnp.bfloat16):
    blocks, slots = tiles.shape
    keys = slots * BLOCK
    width = k3.shape[-1]
    grid_spec = pltpu.PrefetchScalarGridSpec(
        num_scalar_prefetch=2,
        grid=(blocks,),
        in_specs=[
            pl.BlockSpec(memory_space=pltpu.VMEM),
            pl.BlockSpec(memory_space=pltpu.VMEM),
            pl.BlockSpec((1, BLOCK, width), lambda b, c, t: (b, 0, 0)),
            pl.BlockSpec((1, BLOCK, width), lambda b, c, t: (b, 0, 0)),
            pl.BlockSpec((1, BLOCK, 2 * width), lambda b, c, t: (b, 0, 0)),
        ],
        out_specs=[
            pl.BlockSpec((1, BLOCK, width), lambda b, c, t: (b, 0, 0)),
            pl.BlockSpec((1, BLOCK, width), lambda b, c, t: (b, 0, 0)),
        ],
    )
    flops = blocks * (width // 128) * 2 * 4 * 2 * BLOCK * 128 * keys
    cost = pl.CostEstimate(flops=flops, transcendentals=blocks * HEADS * BLOCK * keys,
                           bytes_accessed=qg_blocks.size * 2 + st.size * 4 + 6 * blocks * BLOCK * width * 4)
    return pl.pallas_call(
        functools.partial(key_side_kernel, scale=scale),
        grid_spec=grid_spec,
        out_shape=[jax.ShapeDtypeStruct((blocks, BLOCK, width), out_dtype)] * 2,
        cost_estimate=cost,
    )(tile_count, tiles, qg_blocks, st, k3, v3, returned)


def doubling_gather(x, axis):
    size = lax.axis_size(axis)
    me = lax.axis_index(axis)
    bits = size.bit_length() - 1
    step = size // 2
    while step >= 1:
        other = lax.ppermute(x, axis, [(i, i ^ step) for i in range(size)])
        x = jnp.where((me & step) == 0, jnp.concatenate([x, other], 0), jnp.concatenate([other, x], 0))
        step //= 2
    pieces = x.reshape((2,) * bits + (x.shape[0] // size,) + x.shape[1:])
    order = tuple(reversed(range(bits))) + tuple(range(bits, pieces.ndim))
    return jnp.transpose(pieces, order).reshape(x.shape)


def shards(query, key, value, out_grad, partner, tiles, tile_count):
    f32 = jnp.float32
    bf16 = jnp.bfloat16
    nodes, width = query.shape
    head_dim = width // HEADS
    scale = head_dim ** (-0.5)
    blocks_dev = nodes // BLOCK
    team = lax.axis_size("blk")
    cluster_blocks = blocks_dev * team

    both = jnp.concatenate([key, value], 1)
    kv_cluster = lax.all_gather(both, "blk", axis=0, tiled=True)
    qg_cluster = lax.all_gather(jnp.concatenate([query, out_grad], 1), "blk", axis=0, tiled=True)
    partner_rows = jnp.stack(
        [fetch_partners(both, partner[step], step + 1) for step in range(ROUNDS)]
    )

    out_full, query_grad, terms, stats = query_side(
        tile_count,
        tiles,
        kv_cluster.reshape(cluster_blocks, BLOCK, 2 * width),
        query.reshape(blocks_dev, BLOCK, width),
        out_grad.reshape(blocks_dev, BLOCK, width),
        partner_rows.reshape(ROUNDS, blocks_dev, BLOCK, 2 * width),
        scale,
    )

    stats = stats[..., : 3 * HEADS].reshape(blocks_dev, BLOCK, 3, HEADS)
    stats = jnp.transpose(stats, (0, 2, 3, 1)).reshape(blocks_dev * 3 * HEADS, BLOCK)
    stats_cluster = doubling_gather(stats, "blk")

    terms = terms.reshape(ROUNDS, nodes, 2 * width)
    returned = jnp.stack(
        [fetch_partners(terms[step], partner[step], step + 1) for step in range(ROUNDS)]
    )
    returned = jnp.sum(returned.astype(f32), 0)

    k3 = key.reshape(blocks_dev, BLOCK, width)
    v3 = value.reshape(blocks_dev, BLOCK, width)
    own = jnp.arange(blocks_dev, dtype=jnp.int32)[:, None]
    k_own, v_own = key_side(
        tile_count,
        own,
        jnp.concatenate([query, out_grad], 1).reshape(blocks_dev, BLOCK, 2 * width),
        stats.reshape(blocks_dev, 3, HEADS, BLOCK),
        k3,
        v3,
        jnp.zeros((blocks_dev, BLOCK, 2 * width), f32),
        scale,
        out_dtype=f32,
    )
    returned = returned.reshape(blocks_dev, BLOCK, 2 * width) + jnp.concatenate([k_own, v_own], 2)
    returned, stats_cluster, qg_cluster = lax.optimization_barrier(
        (returned, stats_cluster, qg_cluster)
    )
    key_grad, value_grad = key_side(
        tile_count - 1,
        tiles[:, 1:],
        qg_cluster.reshape(cluster_blocks, BLOCK, 2 * width),
        stats_cluster.reshape(cluster_blocks, 3, HEADS, BLOCK),
        k3,
        v3,
        returned,
        scale,
    )

    attended = out_full.reshape(nodes, width).astype(bf16)
    query_grad = query_grad.reshape(nodes, width)
    key_grad = key_grad.reshape(nodes, width)
    value_grad = value_grad.reshape(nodes, width)
    return (attended, query_grad, key_grad, value_grad)


def solution(mesh):
    in_specs = (
        P(("grp", "blk"), None),
        P(("grp", "blk"), None),
        P(("grp", "blk"), None),
        P(("grp", "blk"), None),
        P(None, ("grp", "blk")),
        P(("grp", "blk"), None),
        P(("grp", "blk")),
    )
    out_specs = (
        P(("grp", "blk"), None),
        P(("grp", "blk"), None),
        P(("grp", "blk"), None),
        P(("grp", "blk"), None),
    )
    return jax.shard_map(shards, mesh=mesh, in_specs=in_specs, out_specs=out_specs, check_vma=False)
```

```python
import functools

import jax
import jax.numpy as jnp
from jax import lax
from jax.experimental import pallas as pl
from jax.experimental.pallas import tpu as pltpu
from jax.sharding import PartitionSpec as P

HEADS = 8
BLOCK = 128
TMAX = 6
ROUNDS = 2


NEG_BIG = -1e30


def passed_along(x, axis, by):
    size = lax.axis_size(axis)
    return lax.ppermute(x, axis, [(i, (i + by) % size) for i in range(size)])


def fetch_partners(load, slots, offset):
    half = load.shape[0] // 2
    ahead = passed_along(load[half:], "grp", -offset)
    behind = passed_along(load[:half], "grp", offset)
    return jnp.concatenate([ahead[slots[:half]], behind[slots[half:]]], 0)


def query_side_kernel(
    count_ref, tiles_ref, kv_ref, q_ref, g_ref, pair_ref, out_ref, qgrad_ref, term_ref, st_ref, *, scale
):
    b = pl.program_id(0)
    width = q_ref.shape[-1]
    slots = tiles_ref.shape[1]
    keys = slots * BLOCK
    ids = [tiles_ref[b, t] for t in range(slots)]
    pair = 2 * (width // HEADS)
    half = pair // 2
    f32, bf16 = jnp.float32, jnp.bfloat16
    live = (lax.broadcasted_iota(jnp.int32, (1, keys), 1) // BLOCK) < count_ref[b]
    low = lax.broadcasted_iota(jnp.int32, (1, pair), 1) < half
    lane = lax.broadcasted_iota(jnp.int32, (1, pair), 1)
    nt = (((1,), (1,)), ((), ()))
    stats = jnp.zeros((BLOCK, pair), f32)
    for pr in range(width // pair):
        cols = pl.ds(pr * pair, pair)
        qp = q_ref[0, :, cols]
        gp = g_ref[0, :, cols]
        kp = jnp.concatenate([kv_ref[i, :, cols] for i in ids], 0)
        vp = jnp.concatenate([kv_ref[i, :, pl.ds(width + pr * pair, pair)] for i in ids], 0)
        kr = [pair_ref[r, 0, :, cols].astype(f32) for r in range(ROUNDS)]
        vr = [pair_ref[r, 0, :, pl.ds(width + pr * pair, pair)].astype(f32) for r in range(ROUNDS)]
        qf = qp.astype(f32)
        gf = gp.astype(f32)
        outs, grads = [], []
        tk = [[] for _ in range(ROUNDS)]
        tv = [[] for _ in range(ROUNDS)]
        for side in range(2):
            mine = low if side == 0 else jnp.logical_not(low)
            h = 2 * pr + side
            qh = jnp.where(mine, qp, jnp.zeros_like(qp))
            gh = jnp.where(mine, gp, jnp.zeros_like(gp))
            qhf = jnp.where(mine, qf, 0.0)
            ghf = jnp.where(mine, gf, 0.0)
            s_loc = lax.dot_general(qh, kp, nt, preferred_element_type=f32) * scale
            s_loc = jnp.where(live, s_loc, NEG_BIG)
            s_pair = [jnp.sum(qhf * kr[r], -1, keepdims=True) * scale for r in range(ROUNDS)]
            top = jnp.max(s_loc, -1, keepdims=True)
            for r in range(ROUNDS):
                top = jnp.maximum(top, s_pair[r])
            e_loc = jnp.exp(s_loc - top)
            e_pair = [jnp.exp(s_pair[r] - top) for r in range(ROUNDS)]
            total = jnp.sum(e_loc, -1, keepdims=True)
            for r in range(ROUNDS):
                total = total + e_pair[r]
            p_loc = e_loc / total
            p_pair = [e_pair[r] / total for r in range(ROUNDS)]
            w_loc = p_loc.astype(bf16)
            w_pair = [p_pair[r].astype(bf16).astype(f32) for r in range(ROUNDS)]
            out = jnp.dot(w_loc, vp, preferred_element_type=f32)
            for r in range(ROUNDS):
                out = out + w_pair[r] * vr[r]
            delta = jnp.sum(jnp.where(mine, gf * out, 0.0), -1, keepdims=True)
            d_loc = lax.dot_general(gh, vp, nt, preferred_element_type=f32)
            d_pair = [jnp.sum(ghf * vr[r], -1, keepdims=True) for r in range(ROUNDS)]
            z_loc = (p_loc * (d_loc - delta)).astype(bf16)
            z_pair = [(p_pair[r] * (d_pair[r] - delta)).astype(bf16).astype(f32) for r in range(ROUNDS)]
            grad = jnp.dot(z_loc, kp, preferred_element_type=f32)
            for r in range(ROUNDS):
                grad = grad + z_pair[r] * kr[r]
            outs.append(out)
            grads.append(grad * scale)
            for r in range(ROUNDS):
                tk[r].append(z_pair[r] * qf * scale)
                tv[r].append(w_pair[r] * gf)
            for i, value in enumerate((top, total, delta)):
                stats = jnp.where(lane == i * HEADS + h, value, stats)
        out_ref[0, :, cols] = jnp.where(low, outs[0], outs[1])
        qgrad_ref[0, :, cols] = jnp.where(low, grads[0], grads[1]).astype(bf16)
        for r in range(ROUNDS):
            term_ref[r, 0, :, cols] = jnp.where(low, tk[r][0], tk[r][1]).astype(bf16)
            term_ref[r, 0, :, pl.ds(width + pr * pair, pair)] = jnp.where(low, tv[r][0], tv[r][1]).astype(bf16)
    st_ref[0] = stats


def query_side(tile_count, tiles, kv_blocks, q3, g3, pair_rows, scale):
    blocks, slots = tiles.shape
    keys = slots * BLOCK
    width2 = kv_blocks.shape[-1]
    width = width2 // 2
    grid_spec = pltpu.PrefetchScalarGridSpec(
        num_scalar_prefetch=2,
        grid=(blocks,),
        in_specs=[
            pl.BlockSpec(memory_space=pltpu.VMEM),
            pl.BlockSpec((1, BLOCK, width), lambda b, c, t: (b, 0, 0)),
            pl.BlockSpec((1, BLOCK, width), lambda b, c, t: (b, 0, 0)),
            pl.BlockSpec((ROUNDS, 1, BLOCK, width2), lambda b, c, t: (0, b, 0, 0)),
        ],
        out_specs=[
            pl.BlockSpec((1, BLOCK, width), lambda b, c, t: (b, 0, 0)),
            pl.BlockSpec((1, BLOCK, width), lambda b, c, t: (b, 0, 0)),
            pl.BlockSpec((ROUNDS, 1, BLOCK, width2), lambda b, c, t: (0, b, 0, 0)),
            pl.BlockSpec((1, BLOCK, 2 * (width // HEADS)), lambda b, c, t: (b, 0, 0)),
        ],
    )
    flops = blocks * (width // 128) * 2 * 4 * 2 * BLOCK * 128 * keys
    cost = pl.CostEstimate(flops=flops, transcendentals=blocks * HEADS * BLOCK * keys,
                           bytes_accessed=kv_blocks.size * 2 + pair_rows.size * 2 + 8 * blocks * BLOCK * width * 4)
    return pl.pallas_call(
        functools.partial(query_side_kernel, scale=scale),
        grid_spec=grid_spec,
        out_shape=[
            jax.ShapeDtypeStruct((blocks, BLOCK, width), jnp.float32),
            jax.ShapeDtypeStruct((blocks, BLOCK, width), jnp.bfloat16),
            jax.ShapeDtypeStruct((ROUNDS, blocks, BLOCK, width2), jnp.bfloat16),
            jax.ShapeDtypeStruct((blocks, BLOCK, 2 * (width // HEADS)), jnp.float32),
        ],
        cost_estimate=cost,
    )(tile_count, tiles, kv_blocks, q3, g3, pair_rows)


def key_side_kernel(count_ref, tiles_ref, qg_ref, st_ref, k_ref, v_ref, ret_ref, ks_ref, vs_ref, *, scale):
    b = pl.program_id(0)
    width = k_ref.shape[-1]
    slots = tiles_ref.shape[1]
    keys = slots * BLOCK
    ids = [tiles_ref[b, t] for t in range(slots)]
    pair = 2 * (width // HEADS)
    half = pair // 2
    live = (lax.broadcasted_iota(jnp.int32, (1, keys), 1) // BLOCK) < count_ref[b]
    low = lax.broadcasted_iota(jnp.int32, (1, pair), 1) < half
    nt = (((1,), (1,)), ((), ()))
    for pr in range(width // pair):
        cols = pl.ds(pr * pair, pair)
        kp = k_ref[0, :, cols]
        vp = v_ref[0, :, cols]
        qp = jnp.concatenate([qg_ref[i, :, cols] for i in ids], 0)
        gp = jnp.concatenate([qg_ref[i, :, pl.ds(width + pr * pair, pair)] for i in ids], 0)
        zero = jnp.zeros_like(kp)
        k_out = []
        v_out = []
        for side in range(2):
            mine = low if side == 0 else jnp.logical_not(low)
            h = 2 * pr + side
            kh = jnp.where(mine, kp, zero)
            vh = jnp.where(mine, vp, zero)
            s = lax.dot_general(kh, qp, nt, preferred_element_type=jnp.float32) * scale
            d = lax.dot_general(vh, gp, nt, preferred_element_type=jnp.float32)
            top, total, delta = [
                jnp.concatenate([st_ref[i, j, pl.ds(h, 1), :] for i in ids], 1) for j in range(3)
            ]
            p = jnp.where(live, jnp.exp(s - top) * (1.0 / total), 0.0)
            w = p.astype(jnp.bfloat16)
            z = (p * (d - delta)).astype(jnp.bfloat16)
            k_out.append(jnp.dot(z, qp, preferred_element_type=jnp.float32))
            v_out.append(jnp.dot(w, gp, preferred_element_type=jnp.float32))
        k_sum = jnp.where(low, k_out[0], k_out[1]) * scale
        v_sum = jnp.where(low, v_out[0], v_out[1])
        ks_ref[0, :, cols] = (k_sum + ret_ref[0, :, cols]).astype(ks_ref.dtype)
        vs_ref[0, :, cols] = (v_sum + ret_ref[0, :, pl.ds(width + pr * pair, pair)]).astype(vs_ref.dtype)


def key_side(tile_count, tiles, qg_blocks, st, k3, v3, returned, scale):
    blocks, slots = tiles.shape
    keys = slots * BLOCK
    width = k3.shape[-1]
    grid_spec = pltpu.PrefetchScalarGridSpec(
        num_scalar_prefetch=2,
        grid=(blocks,),
        in_specs=[
            pl.BlockSpec(memory_space=pltpu.VMEM),
            pl.BlockSpec(memory_space=pltpu.VMEM),
            pl.BlockSpec((1, BLOCK, width), lambda b, c, t: (b, 0, 0)),
            pl.BlockSpec((1, BLOCK, width), lambda b, c, t: (b, 0, 0)),
            pl.BlockSpec((1, BLOCK, 2 * width), lambda b, c, t: (b, 0, 0)),
        ],
        out_specs=[
            pl.BlockSpec((1, BLOCK, width), lambda b, c, t: (b, 0, 0)),
            pl.BlockSpec((1, BLOCK, width), lambda b, c, t: (b, 0, 0)),
        ],
    )
    flops = blocks * (width // 128) * 2 * 4 * 2 * BLOCK * 128 * keys
    cost = pl.CostEstimate(flops=flops, transcendentals=blocks * HEADS * BLOCK * keys,
                           bytes_accessed=qg_blocks.size * 2 + st.size * 4 + 6 * blocks * BLOCK * width * 4)
    return pl.pallas_call(
        functools.partial(key_side_kernel, scale=scale),
        grid_spec=grid_spec,
        out_shape=[jax.ShapeDtypeStruct((blocks, BLOCK, width), jnp.bfloat16)] * 2,
        cost_estimate=cost,
    )(tile_count, tiles, qg_blocks, st, k3, v3, returned)


def doubling_gather(x, axis):
    size = lax.axis_size(axis)
    me = lax.axis_index(axis)
    bits = size.bit_length() - 1
    step = size // 2
    while step >= 1:
        other = lax.ppermute(x, axis, [(i, i ^ step) for i in range(size)])
        x = jnp.where((me & step) == 0, jnp.concatenate([x, other], 0), jnp.concatenate([other, x], 0))
        step //= 2
    pieces = x.reshape((2,) * bits + (x.shape[0] // size,) + x.shape[1:])
    order = tuple(reversed(range(bits))) + tuple(range(bits, pieces.ndim))
    return jnp.transpose(pieces, order).reshape(x.shape)


def shards(query, key, value, out_grad, partner, tiles, tile_count):
    f32 = jnp.float32
    bf16 = jnp.bfloat16
    nodes, width = query.shape
    head_dim = width // HEADS
    scale = head_dim ** (-0.5)
    blocks_dev = nodes // BLOCK
    team = lax.axis_size("blk")
    cluster_blocks = blocks_dev * team

    both = jnp.concatenate([key, value], 1)
    kv_cluster = lax.all_gather(both, "blk", axis=0, tiled=True)
    qg_cluster = lax.all_gather(jnp.concatenate([query, out_grad], 1), "blk", axis=0, tiled=True)
    partner_rows = jnp.stack(
        [fetch_partners(both, partner[step], step + 1) for step in range(ROUNDS)]
    )

    out_full, query_grad, terms, stats = query_side(
        tile_count,
        tiles,
        kv_cluster.reshape(cluster_blocks, BLOCK, 2 * width),
        query.reshape(blocks_dev, BLOCK, width),
        out_grad.reshape(blocks_dev, BLOCK, width),
        partner_rows.reshape(ROUNDS, blocks_dev, BLOCK, 2 * width),
        scale,
    )

    stats = stats[..., : 3 * HEADS].reshape(blocks_dev, BLOCK, 3, HEADS)
    stats = jnp.transpose(stats, (0, 2, 3, 1)).reshape(blocks_dev * 3 * HEADS, BLOCK)
    stats_cluster = doubling_gather(stats, "blk")

    terms = terms.reshape(ROUNDS, nodes, 2 * width)
    returned = jnp.stack(
        [fetch_partners(terms[step], partner[step], step + 1) for step in range(ROUNDS)]
    )
    returned = jnp.sum(returned.astype(f32), 0)
    returned, stats_cluster, qg_cluster = lax.optimization_barrier(
        (returned, stats_cluster, qg_cluster)
    )

    key_grad, value_grad = key_side(
        tile_count,
        tiles,
        qg_cluster.reshape(cluster_blocks, BLOCK, 2 * width),
        stats_cluster.reshape(cluster_blocks, 3, HEADS, BLOCK),
        key.reshape(blocks_dev, BLOCK, width),
        value.reshape(blocks_dev, BLOCK, width),
        returned.reshape(blocks_dev, BLOCK, 2 * width),
        scale,
    )

    attended = out_full.reshape(nodes, width).astype(bf16)
    query_grad = query_grad.reshape(nodes, width)
    key_grad = key_grad.reshape(nodes, width)
    value_grad = value_grad.reshape(nodes, width)
    return (attended, query_grad, key_grad, value_grad)


def solution(mesh):
    in_specs = (
        P(("grp", "blk"), None),
        P(("grp", "blk"), None),
        P(("grp", "blk"), None),
        P(("grp", "blk"), None),
        P(None, ("grp", "blk")),
        P(("grp", "blk"), None),
        P(("grp", "blk")),
    )
    out_specs = (
        P(("grp", "blk"), None),
        P(("grp", "blk"), None),
        P(("grp", "blk"), None),
        P(("grp", "blk"), None),
    )
    return jax.shard_map(shards, mesh=mesh, in_specs=in_specs, out_specs=out_specs, check_vma=False)
```
